256 devices in a mesh: ctx: 64 (over x, z, core), tp: 4 (over y).
Axes of the slice: x: 4, y: 4, z: 8, core: 2. Of those that a mesh axis runs over, the one named last changes fastest.
Arguments:
- inputs: bfloat16 [8192, 4096], P('ctx'), may hold values from -6 to 6
- w_query: bfloat16 [4096, 4096], P(None, 'tp'), may hold values from -0.109375 to 0.109375
- w_key: bfloat16 [4096, 512], P(None, 'tp'), may hold values from -0.109375 to 0.109375
- w_value: bfloat16 [4096, 512], P(None, 'tp'), may hold values from -0.09375 to 0.09375
- attn_out: bfloat16 [8192, 4096], P('ctx', 'tp'), may hold values from -6 to 6
- d_out: bfloat16 [8192, 4096], P('ctx', 'tp'), may hold values from -6 to 6
- block_order: int32 [128], replicated, may hold values from 0 to 127, each once
Outputs:
- d_input: bfloat16 [8192, 4096], P('ctx', 'tp')
The draws below stay inside these ranges and needn't reach their ends.
Inputs may be any that keep to these rules, and one draw needn't show every extreme that they name: `block_order`: a permutation of the sequence blocks.
All inputs are finite; a program needn't handle non-finite values.
Results may differ from the reference program's by a relative error of at most 0.012.
Values may be sent and summed in bfloat16 or wider, within the bound.
No kernel may reach another device: no remote copies, remote signals or barrier semaphores. Data moves between devices by JAX's collectives and lax.ppermute only.
A program may use at most 192 MiB of HBM per device.

```python
import jax
import jax.numpy as jnp
from jax import lax

D = 4096
HEADS = 32
KV_HEADS = 4
HD = 128
TOK_DEV = 128
BLOCKS = 128
SEQ = 8192


def draw_w_key(key, part):
    noise = jnp.clip(jax.random.normal(jax.random.fold_in(key, 7102), (D, KV_HEADS * HD), jnp.float32), -6.0, 6.0) * D ** (-0.5)
    return noise.astype(jnp.bfloat16)


def draw_w_query(key, part):
    noise = jnp.clip(jax.random.normal(jax.random.fold_in(key, 7101), (D, HEADS * HD), jnp.float32), -6.0, 6.0) * D ** (-0.5)
    return noise.astype(jnp.bfloat16)


def draw_inputs(key, part):
    field = jnp.clip(jax.random.normal(jax.random.fold_in(key, 7201), (SEQ, D), jnp.float32), -6.0, 6.0)
    return field.astype(jnp.bfloat16)


def shard_levels(stream_key, dims, shards, least, high):
    def one(axis_at, parts):
        heights = jax.random.uniform(jax.random.fold_in(jax.random.fold_in(stream_key, 6), axis_at), (parts,), jnp.float32, least / len(shards), high / len(shards))
        return jnp.repeat(jnp.exp(heights), dims[axis_at] // parts).reshape((-1,) + (1,) * (len(dims) - axis_at - 1))

    level = one(*shards[0])
    for cut in shards[1:]:
        level = level * one(*cut)
    return level


def bell_draw(key, extent, scale, bound, cuts=(), held_as=jnp.bfloat16):
    values = jax.random.normal(key, extent, jnp.float32) * scale
    if len(cuts) > 0:
        values = shard_levels(key, extent, cuts, -0.22, 0.18) * values
    return jnp.clip(values, min=-bound, max=bound).astype(held_as)


def setup_inputs(seed: int = 0) -> dict:
    key_list = jax.random.split(jax.random.key(seed), 8)
    return {
        "inputs": draw_inputs(jax.random.fold_in(key_list[7], 71), 0),
        "w_query": draw_w_query(jax.random.fold_in(key_list[7], 71), 0),
        "w_key": draw_w_key(jax.random.fold_in(key_list[7], 71), 0),
        "w_value": bell_draw(key_list[3], (D, KV_HEADS * HD), D ** -0.5, 0.09375, ((1, 4),)),
        "attn_out": bell_draw(key_list[4], (SEQ, HEADS * HD), 1.0, 6.0, ((0, 64), (1, 4))),
        "d_out": bell_draw(key_list[5], (SEQ, HEADS * HD), 1.0, 6.0, ((0, 64), (1, 4))),
        "block_order": jax.random.permutation(key_list[6], BLOCKS).astype(jnp.int32),
    }


def reference(inputs, w_query, w_key, w_value, attn_out, d_out, block_order):
    seq = inputs.shape[0]
    span = TOK_DEV // 2
    rows = jnp.arange(seq, dtype=jnp.int32)
    pos = block_order[rows // span] * span + rows % span
    scale = HD ** -0.5
    group = HEADS // KV_HEADS
    queries = jnp.dot(inputs, w_query, preferred_element_type=jnp.float32).astype(jnp.bfloat16).reshape(seq, HEADS, HD)
    keys = jnp.dot(inputs, w_key, preferred_element_type=jnp.float32).astype(jnp.bfloat16).reshape(seq, KV_HEADS, HD)
    values = jnp.dot(inputs, w_value, preferred_element_type=jnp.float32).astype(jnp.bfloat16).reshape(seq, KV_HEADS, HD)
    grads3 = d_out.reshape(seq, HEADS, HD)
    outs3 = attn_out.reshape(seq, HEADS, HD)
    delta = jnp.sum(grads3.astype(jnp.float32) * outs3.astype(jnp.float32), axis=-1)
    qblock = min(1024, seq)
    nblock = seq // qblock

    def per_group(g):
        qg = lax.dynamic_slice_in_dim(queries, g * group, group, 1).astype(jnp.float32)
        dg = lax.dynamic_slice_in_dim(grads3, g * group, group, 1).astype(jnp.float32)
        eg = lax.dynamic_slice_in_dim(delta, g * group, group, 1)
        kg = lax.dynamic_index_in_dim(keys, g, 1, keepdims=False).astype(jnp.float32)
        vg = lax.dynamic_index_in_dim(values, g, 1, keepdims=False).astype(jnp.float32)

        def step(carry, b):
            dk, dv = carry
            start = b * qblock
            qs = lax.dynamic_slice_in_dim(qg, start, qblock, 0)
            ds_rows = lax.dynamic_slice_in_dim(dg, start, qblock, 0)
            es = lax.dynamic_slice_in_dim(eg, start, qblock, 0)
            ps = lax.dynamic_slice_in_dim(pos, start, qblock, 0)
            mask = pos[None, :] <= ps[:, None]
            s = jnp.einsum('thd,nd->htn', qs, kg) * scale
            s = jnp.where(mask[None], s, -jnp.inf)
            top = jnp.max(s, axis=-1, keepdims=True)
            lse = top + jnp.log(jnp.sum(jnp.exp(s - top), axis=-1, keepdims=True))
            p = jnp.where(mask[None], jnp.exp(s - lse), 0.0)
            dp = jnp.einsum('thd,nd->htn', ds_rows, vg)
            dsc = p * (dp - es.T[:, :, None])
            ds_b = (dsc * scale).astype(jnp.bfloat16).astype(jnp.float32)
            p_b = p.astype(jnp.bfloat16).astype(jnp.float32)
            dq = jnp.einsum('htn,nd->thd', ds_b, kg)
            dk = dk + jnp.einsum('htn,thd->nd', ds_b, qs)
            dv = dv + jnp.einsum('htn,thd->nd', p_b, ds_rows)
            return (dk, dv), dq

        zero = jnp.zeros((seq, HD), jnp.float32)
        (dk, dv), dq = lax.scan(step, (zero, zero), jnp.arange(nblock, dtype=jnp.int32))
        return dq.reshape(seq, group, HD), dk, dv

    dq, dk, dv = lax.map(per_group, jnp.arange(KV_HEADS, dtype=jnp.int32))
    dq_b = jnp.transpose(dq, (1, 0, 2, 3)).reshape(seq, HEADS * HD).astype(jnp.bfloat16)
    dk_b = jnp.transpose(dk, (1, 0, 2)).reshape(seq, KV_HEADS * HD).astype(jnp.bfloat16)
    dv_b = jnp.transpose(dv, (1, 0, 2)).reshape(seq, KV_HEADS * HD).astype(jnp.bfloat16)
    total = jnp.dot(dq_b, w_query.T, preferred_element_type=jnp.float32)
    total = total + jnp.dot(dk_b, w_key.T, preferred_element_type=jnp.float32)
    total = total + jnp.dot(dv_b, w_value.T, preferred_element_type=jnp.float32)
    return total.astype(jnp.bfloat16)
```

```python
import math

import numpy as np

import jax
import jax.numpy as jnp
from jax import lax
from jax.sharding import PartitionSpec as P

big_negative = -1e30


def exchange_orders(n):
    if n == 64:
        return ([5, 3, 2, 4, 1, 0], [3, 2, 5, 1, 4, 0])
    bits = list(range(int(math.log2(n))))[::-1]
    return (bits, bits)


def step_partners(n, orders, s):
    return [i ^ (1 << orders[i & 1][s]) for i in range(n)]


def owner_table(n, orders):
    owners = [[i] for i in range(n)]
    for s in range(len(orders[0])):
        partner = step_partners(n, orders, s)
        owners = [owners[i] + owners[partner[i]] for i in range(n)]
    return np.asarray(owners, np.int32)


def gather_slots(pieces, n, orders):
    bufs = tuple(p[None] for p in pieces)
    for s in range(len(orders[0])):
        partner = step_partners(n, orders, s)
        other = lax.ppermute(bufs, "ctx", [(i, partner[i]) for i in range(n)])
        bufs = tuple(jnp.concatenate([b, o], axis=0) for b, o in zip(bufs, other))
    return bufs


def scatter_slots(bufs, n, orders):
    for s in reversed(range(len(orders[0]))):
        partner = step_partners(n, orders, s)
        half = bufs[0].shape[0] // 2
        recv = lax.ppermute(
            tuple(b[half:] for b in bufs), "ctx", [(i, partner[i]) for i in range(n)]
        )
        bufs = tuple(b[:half] + r for b, r in zip(bufs, recv))
    return tuple(b[0] for b in bufs)


def row_positions(order, start, count, span):
    rows = start + lax.iota(jnp.int32, count)
    slot = rows // span
    table = jnp.sum(
        jnp.where(slot[:, None] == lax.iota(jnp.int32, order.shape[0])[None, :], order[None, :], 0),
        axis=1,
    )
    return table * span + rows % span


def contract_rows(left, weight):
    return lax.dot_general(
        left, weight, (((1,), (1,)), ((), ())), preferred_element_type=jnp.float32
    )


def on_device(inputs, w_query, w_key, w_value, attn_out, d_out, block_order):
    tokens = inputs.shape[0]
    span = tokens // 2
    head_dim = w_key.shape[1]
    heads = w_query.shape[1] // head_dim
    scale = head_dim ** (-0.5)
    n = lax.axis_size("ctx")
    orders = exchange_orders(n)
    me = lax.axis_index("ctx")
    keys = jnp.dot(inputs, w_key, preferred_element_type=jnp.float32).astype(jnp.bfloat16)
    values = jnp.dot(inputs, w_value, preferred_element_type=jnp.float32).astype(jnp.bfloat16)
    seq = tokens * n
    my_pos = row_positions(block_order, me * tokens, tokens, span)
    latest = jnp.max(my_pos)
    queries = (
        jnp.dot(inputs, w_query, preferred_element_type=jnp.float32)
        .astype(jnp.bfloat16)
        .reshape(tokens, heads, head_dim)
    )
    grads3 = d_out.reshape(tokens, heads, head_dim)
    delta = jnp.sum(
        grads3.astype(jnp.float32) * attn_out.reshape(tokens, heads, head_dim).astype(jnp.float32),
        axis=-1,
    ).T

    owners = lax.dynamic_index_in_dim(jnp.asarray(owner_table(n, orders)), me, 0, keepdims=False)
    local_rows = lax.iota(jnp.int32, tokens)
    key_rows = owners[:, None] * tokens + local_rows[None, :]
    all_pos = (jnp.take(block_order, key_rows // span) * span + key_rows % span).reshape(seq)

    def guarded(work, carry, start, count):
        key_pos = lax.dynamic_slice_in_dim(all_pos, start, count, 0)
        return lax.cond(jnp.min(key_pos) > latest, lambda c: c, lambda c: work(c, key_pos), carry)

    def stats_step(carry, piece_k, start):

        def work(state, key_pos):
            top, total = state
            mask = (key_pos[None, :] <= my_pos[:, None])[None]
            s = (
                jnp.einsum("thd,nd->htn", queries, piece_k, preferred_element_type=jnp.float32)
                * scale
            )
            s = jnp.where(mask, s, big_negative)
            top_new = jnp.maximum(top, jnp.max(s, axis=-1))
            terms = jnp.where(mask, jnp.exp(s - top_new[..., None]), 0.0)
            return (top_new, total * jnp.exp(top - top_new) + jnp.sum(terms, axis=-1))

        return guarded(work, carry, start, piece_k.shape[0])

    def grad_step(carry, pieces, start):
        piece_k, piece_v = pieces

        def work(state, key_pos):
            dq, dk_full, dv_full = state
            mask = (key_pos[None, :] <= my_pos[:, None])[None]
            s = (
                jnp.einsum("thd,nd->htn", queries, piece_k, preferred_element_type=jnp.float32)
                * scale
            )
            p = jnp.where(mask, jnp.exp(s - lse[..., None]), 0.0)
            dp = jnp.einsum("thd,nd->htn", grads3, piece_v, preferred_element_type=jnp.float32)
            ds_b = (p * (dp - delta[..., None]) * scale).astype(jnp.bfloat16)
            p_b = p.astype(jnp.bfloat16)
            dq = dq + jnp.einsum("htn,nd->thd", ds_b, piece_k, preferred_element_type=jnp.float32)
            dk_piece = jnp.einsum("htn,thd->nd", ds_b, queries, preferred_element_type=jnp.float32)
            dv_piece = jnp.einsum("htn,thd->nd", p_b, grads3, preferred_element_type=jnp.float32)
            dk_full = lax.dynamic_update_slice_in_dim(dk_full, dk_piece, start, 0)
            dv_full = lax.dynamic_update_slice_in_dim(dv_full, dv_piece, start, 0)
            return (dq, dk_full, dv_full)

        return guarded(work, carry, start, piece_k.shape[0])

    stats_init = (
        jnp.full((heads, tokens), big_negative, jnp.float32),
        jnp.zeros((heads, tokens), jnp.float32),
    )
    zero_rows = jnp.zeros((seq, head_dim), jnp.float32)
    grad_init = (jnp.zeros((tokens, heads, head_dim), jnp.float32), zero_rows, zero_rows)
    slot_keys, slot_values = gather_slots((keys, values), n, orders)
    all_keys = slot_keys.reshape(seq, head_dim)
    all_values = slot_values.reshape(seq, head_dim)
    block = math.gcd(seq, 1024)
    count = seq // block

    def stats_loop(i, state):
        start = (i * block).astype(jnp.int32)
        return stats_step(state, lax.dynamic_slice_in_dim(all_keys, start, block, 0), start)

    top, total = lax.fori_loop(0, count, stats_loop, stats_init)
    lse = top + jnp.log(total)

    def grad_loop(i, state):
        start = (i * block).astype(jnp.int32)
        pieces = (
            lax.dynamic_slice_in_dim(all_keys, start, block, 0),
            lax.dynamic_slice_in_dim(all_values, start, block, 0),
        )
        return grad_step(state, pieces, start)

    dq, dk_full, dv_full = lax.fori_loop(0, count, grad_loop, grad_init)
    dk_mine, dv_mine = scatter_slots(
        (dk_full.reshape(n, tokens, head_dim), dv_full.reshape(n, tokens, head_dim)), n, orders
    )
    dq_b = dq.astype(jnp.bfloat16).reshape(tokens, heads * head_dim)
    partial_value = contract_rows(dq_b, w_query)
    partial_value = partial_value + contract_rows(dk_mine.astype(jnp.bfloat16), w_key)
    partial_value = partial_value + contract_rows(dv_mine.astype(jnp.bfloat16), w_value)
    return lax.psum_scatter(
        partial_value.astype(jnp.bfloat16), "tp", scatter_dimension=1, tiled=True
    )


def solution(mesh):
    placed = (
        P("ctx", None),
        P(None, "tp"),
        P(None, "tp"),
        P(None, "tp"),
        P("ctx", "tp"),
        P("ctx", "tp"),
        P(),
    )
    return jax.shard_map(
        on_device, mesh=mesh, in_specs=placed, out_specs=P("ctx", "tp"), check_vma=False
    )
```

```python
import math

import numpy as np

import jax
import jax.numpy as jnp
from jax import lax
from jax.sharding import PartitionSpec as P

big_negative = -1e30


def exchange_orders(n):
    if n == 64:
        return ([5, 3, 2, 4, 1, 0], [3, 2, 5, 1, 4, 0])
    bits = list(range(int(math.log2(n))))[::-1]
    return (bits, bits)


def step_pairs(n, orders, s):
    return [(i, i ^ (1 << orders[i & 1][s])) for i in range(n)]


def owner_table(n, orders):
    owners = [[i] for i in range(n)]
    for s in range(len(orders[0])):
        owners = [owners[i] + owners[j] for i, j in step_pairs(n, orders, s)]
    return np.asarray(owners, np.int32)


def gather_parts(pieces, n, orders):
    parts = [tuple(p[None] for p in pieces)]
    buf = parts[0]
    for s in range(len(orders[0])):
        other = lax.ppermute(buf, "ctx", step_pairs(n, orders, s))
        parts.append(other)
        if s + 1 < len(orders[0]):
            buf = tuple(jnp.concatenate([b, o], axis=0) for b, o in zip(buf, other))
    return parts


def slot_range(parts, lo, hi):
    picked = []
    for s, part in enumerate(parts):
        first = 0 if s == 0 else 2 ** (s - 1)
        size = part[0].shape[0]
        a, b = max(lo, first), min(hi, first + size)
        if a < b:
            picked.append(tuple(x[a - first : b - first] for x in part))
    if len(picked) == 1:
        return picked[0]
    return tuple(jnp.concatenate(xs, axis=0) for xs in zip(*picked))


def row_positions(order, start, count, span):
    rows = start + lax.iota(jnp.int32, count)
    slot = rows // span
    table = jnp.sum(
        jnp.where(slot[:, None] == lax.iota(jnp.int32, order.shape[0])[None, :], order[None, :], 0),
        axis=1,
    )
    return table * span + rows % span


def contract_rows(left, weight):
    return lax.dot_general(
        left, weight, (((1,), (1,)), ((), ())), preferred_element_type=jnp.float32
    )


def on_device(inputs, w_query, w_key, w_value, attn_out, d_out, block_order):
    tokens = inputs.shape[0]
    span = tokens // 2
    head_dim = w_key.shape[1]
    heads = w_query.shape[1] // head_dim
    scale = head_dim ** (-0.5)
    n = lax.axis_size("ctx")
    orders = exchange_orders(n)
    steps = len(orders[0])
    me = lax.axis_index("ctx")
    keys = jnp.dot(inputs, w_key, preferred_element_type=jnp.float32).astype(jnp.bfloat16)
    values = jnp.dot(inputs, w_value, preferred_element_type=jnp.float32).astype(jnp.bfloat16)
    seq = tokens * n
    my_pos = row_positions(block_order, me * tokens, tokens, span)
    queries = (
        jnp.dot(inputs, w_query, preferred_element_type=jnp.float32)
        .astype(jnp.bfloat16)
        .reshape(tokens, heads, head_dim)
    )
    grads3 = d_out.reshape(tokens, heads, head_dim)
    delta = jnp.sum(
        grads3.astype(jnp.float32) * attn_out.reshape(tokens, heads, head_dim).astype(jnp.float32),
        axis=-1,
    ).T

    owners = lax.dynamic_index_in_dim(jnp.asarray(owner_table(n, orders)), me, 0, keepdims=False)
    per_owner = tokens // span
    owner_blocks = (owners[:, None] * per_owner + lax.iota(jnp.int32, per_owner)[None, :]).reshape(-1)
    block_ids = jnp.sum(
        jnp.where(
            owner_blocks[:, None] == lax.iota(jnp.int32, block_order.shape[0])[None, :],
            block_order[None, :],
            0,
        ),
        axis=1,
    )
    all_pos = (block_ids[:, None] * span + lax.iota(jnp.int32, span)[None, :]).reshape(seq)

    parts = gather_parts((keys, values), n, orders)
    block = math.gcd(seq, 1024)
    count = seq // block
    per_block = block // tokens

    def block_kv(b):
        k, v = slot_range(parts, b * per_block, (b + 1) * per_block)
        return k.reshape(block, head_dim), v.reshape(block, head_dim)

    def block_mask(b):
        key_pos = lax.slice_in_dim(all_pos, b * block, (b + 1) * block)
        return (key_pos[None, :] <= my_pos[:, None])[None]

    top = jnp.full((heads, tokens), big_negative, jnp.float32)
    total = jnp.zeros((heads, tokens), jnp.float32)
    for b in range(count):
        piece_k, _ = block_kv(b)
        mask = block_mask(b)
        s = jnp.einsum("thd,nd->htn", queries, piece_k, preferred_element_type=jnp.float32) * scale
        s = jnp.where(mask, s, big_negative)
        top_new = jnp.maximum(top, jnp.max(s, axis=-1))
        terms = jnp.where(mask, jnp.exp(s - top_new[..., None]), 0.0)
        total = total * jnp.exp(top - top_new) + jnp.sum(terms, axis=-1)
        top = top_new
    lse = top + jnp.log(total)

    dq = jnp.zeros((tokens, heads, head_dim), jnp.float32)
    acc = [None] * count
    for b in reversed(range(count)):
        piece_k, piece_v = block_kv(b)
        mask = block_mask(b)
        s = jnp.einsum("thd,nd->htn", queries, piece_k, preferred_element_type=jnp.float32) * scale
        p = jnp.where(mask, jnp.exp(s - lse[..., None]), 0.0)
        dp = jnp.einsum("thd,nd->htn", grads3, piece_v, preferred_element_type=jnp.float32)
        ds_b = (p * (dp - delta[..., None]) * scale).astype(jnp.bfloat16)
        p_b = p.astype(jnp.bfloat16)
        dq = dq + jnp.einsum("htn,nd->thd", ds_b, piece_k, preferred_element_type=jnp.float32)
        dk_piece = jnp.einsum("htn,thd->nd", ds_b, queries, preferred_element_type=jnp.float32)
        dv_piece = jnp.einsum("htn,thd->nd", p_b, grads3, preferred_element_type=jnp.float32)
        own = (
            dk_piece.reshape(per_block, tokens, head_dim),
            dv_piece.reshape(per_block, tokens, head_dim),
        )
        acc[b] = own if acc[b] is None else tuple(x + y for x, y in zip(own, acc[b]))
        for s_step in reversed(range(steps)):
            lo_block = 2 ** s_step // per_block
            if lo_block == 0:
                break
            if lo_block <= b < 2 * lo_block:
                recv = lax.ppermute(acc[b], "ctx", step_pairs(n, orders, s_step))
                dst = b - lo_block
                acc[dst] = recv if acc[dst] is None else tuple(
                    x + y for x, y in zip(acc[dst], recv)
                )
                acc[b] = None
                break
    last = acc[0]
    for s_step in reversed(range(steps)):
        half = 2 ** s_step
        if half >= per_block:
            continue
        recv = lax.ppermute(
            tuple(x[half : 2 * half] for x in last), "ctx", step_pairs(n, orders, s_step)
        )
        last = tuple(x[:half] + r for x, r in zip(last, recv))
    dk_mine, dv_mine = (x[0] for x in last)

    dq_b = dq.astype(jnp.bfloat16).reshape(tokens, heads * head_dim)
    partial_value = contract_rows(dq_b, w_query)
    partial_value = partial_value + contract_rows(dk_mine.astype(jnp.bfloat16), w_key)
    partial_value = partial_value + contract_rows(dv_mine.astype(jnp.bfloat16), w_value)
    return lax.psum_scatter(
        partial_value.astype(jnp.bfloat16), "tp", scatter_dimension=1, tiled=True
    )


def solution(mesh):
    placed = (
        P("ctx", None),
        P(None, "tp"),
        P(None, "tp"),
        P(None, "tp"),
        P("ctx", "tp"),
        P("ctx", "tp"),
        P(),
    )
    return jax.shard_map(
        on_device, mesh=mesh, in_specs=placed, out_specs=P("ctx", "tp"), check_vma=False
    )
```

```python
import math

import numpy as np

import jax
import jax.numpy as jnp
from jax import lax
from jax.sharding import PartitionSpec as P

big_negative = -1e30


def exchange_orders(n):
    if n == 64:
        return ([5, 3, 2, 4, 1, 0], [3, 2, 5, 1, 4, 0])
    bits = list(range(int(math.log2(n))))[::-1]
    return (bits, bits)


def step_pairs(n, orders, s):
    return [(i, i ^ (1 << orders[i & 1][s])) for i in range(n)]


def owner_table(n, orders):
    owners = [[i] for i in range(n)]
    for s in range(len(orders[0])):
        owners = [owners[i] + owners[j] for i, j in step_pairs(n, orders, s)]
    return np.asarray(owners, np.int32)


def gather_parts(pieces, n, orders):
    parts = [tuple(p[None] for p in pieces)]
    buf = parts[0]
    for s in range(len(orders[0])):
        other = lax.ppermute(buf, "ctx", step_pairs(n, orders, s))
        parts.append(other)
        if s + 1 < len(orders[0]):
            buf = tuple(jnp.concatenate([b, o], axis=0) for b, o in zip(buf, other))
    return parts


def slot_range(parts, lo, hi):
    picked = []
    for s, part in enumerate(parts):
        first = 0 if s == 0 else 2 ** (s - 1)
        size = part[0].shape[0]
        a, b = max(lo, first), min(hi, first + size)
        if a < b:
            picked.append(tuple(x[a - first : b - first] for x in part))
    if len(picked) == 1:
        return picked[0]
    return tuple(jnp.concatenate(xs, axis=0) for xs in zip(*picked))


def row_positions(order, start, count, span):
    rows = start + lax.iota(jnp.int32, count)
    slot = rows // span
    table = jnp.sum(
        jnp.where(slot[:, None] == lax.iota(jnp.int32, order.shape[0])[None, :], order[None, :], 0),
        axis=1,
    )
    return table * span + rows % span


def contract_rows(left, weight):
    return lax.dot_general(
        left, weight, (((1,), (1,)), ((), ())), preferred_element_type=jnp.float32
    )


def on_device(inputs, w_query, w_key, w_value, attn_out, d_out, block_order):
    tokens = inputs.shape[0]
    span = tokens // 2
    head_dim = w_key.shape[1]
    heads = w_query.shape[1] // head_dim
    scale = head_dim ** (-0.5)
    n = lax.axis_size("ctx")
    orders = exchange_orders(n)
    steps = len(orders[0])
    me = lax.axis_index("ctx")
    keys = jnp.dot(inputs, w_key, preferred_element_type=jnp.float32).astype(jnp.bfloat16)
    values = jnp.dot(inputs, w_value, preferred_element_type=jnp.float32).astype(jnp.bfloat16)
    seq = tokens * n
    my_pos = row_positions(block_order, me * tokens, tokens, span)
    queries = (
        jnp.dot(inputs, w_query, preferred_element_type=jnp.float32)
        .astype(jnp.bfloat16)
        .reshape(tokens, heads, head_dim)
    )
    grads3 = d_out.reshape(tokens, heads, head_dim)
    delta = jnp.sum(
        grads3.astype(jnp.float32) * attn_out.reshape(tokens, heads, head_dim).astype(jnp.float32),
        axis=-1,
    ).T

    owners = lax.dynamic_index_in_dim(jnp.asarray(owner_table(n, orders)), me, 0, keepdims=False)
    per_owner = tokens // span
    owner_blocks = (owners[:, None] * per_owner + lax.iota(jnp.int32, per_owner)[None, :]).reshape(-1)
    block_ids = jnp.sum(
        jnp.where(
            owner_blocks[:, None] == lax.iota(jnp.int32, block_order.shape[0])[None, :],
            block_order[None, :],
            0,
        ),
        axis=1,
    )
    all_pos = (block_ids[:, None] * span + lax.iota(jnp.int32, span)[None, :]).reshape(seq)

    m = lax.axis_size("tp")
    t = lax.axis_index("tp")
    cols = w_query.shape[0] // m
    kv_weights = jnp.concatenate([w_key, w_value], axis=1)
    my_kv_rows = lax.dynamic_slice_in_dim(kv_weights, t * cols, cols, 0)
    kv_rows_from = [None]
    for k in range(1, m):
        shift = [(j, (j + k) % m) for j in range(m)]
        sent = lax.dynamic_slice_in_dim(kv_weights, ((t + k) % m) * cols, cols, 0)
        kv_rows_from.append(lax.ppermute(sent, "tp", shift))

    parts = gather_parts((keys, values), n, orders)
    block = math.gcd(seq, 1024)
    count = seq // block
    per_block = block // tokens

    def block_kv(b):
        k, v = slot_range(parts, b * per_block, (b + 1) * per_block)
        return k.reshape(block, head_dim), v.reshape(block, head_dim)

    def block_mask(b):
        key_pos = lax.slice_in_dim(all_pos, b * block, (b + 1) * block)
        return (key_pos[None, :] <= my_pos[:, None])[None]

    top = jnp.full((heads, tokens), big_negative, jnp.float32)
    total = jnp.zeros((heads, tokens), jnp.float32)
    for b in range(count):
        piece_k, _ = block_kv(b)
        mask = block_mask(b)
        s = jnp.einsum("thd,nd->htn", queries, piece_k, preferred_element_type=jnp.float32) * scale
        s = jnp.where(mask, s, big_negative)
        top_new = jnp.maximum(top, jnp.max(s, axis=-1))
        terms = jnp.where(mask, jnp.exp(s - top_new[..., None]), 0.0)
        total = total * jnp.exp(top - top_new) + jnp.sum(terms, axis=-1)
        top = top_new
    lse = top + jnp.log(total)

    dq = jnp.zeros((tokens, heads, head_dim), jnp.float32)
    acc = [None] * count
    for b in reversed(range(count)):
        piece_k, piece_v = block_kv(b)
        mask = block_mask(b)
        s = jnp.einsum("thd,nd->htn", queries, piece_k, preferred_element_type=jnp.float32) * scale
        p = jnp.where(mask, jnp.exp(s - lse[..., None]), 0.0)
        dp = jnp.einsum("thd,nd->htn", grads3, piece_v, preferred_element_type=jnp.float32)
        ds_b = (p * (dp - delta[..., None]) * scale).astype(jnp.bfloat16)
        p_b = p.astype(jnp.bfloat16)
        dq = dq + jnp.einsum("htn,nd->thd", ds_b, piece_k, preferred_element_type=jnp.float32)
        dk_piece = jnp.einsum("htn,thd->nd", ds_b, queries, preferred_element_type=jnp.float32)
        dv_piece = jnp.einsum("htn,thd->nd", p_b, grads3, preferred_element_type=jnp.float32)
        own = (
            dk_piece.reshape(per_block, tokens, head_dim),
            dv_piece.reshape(per_block, tokens, head_dim),
        )
        acc[b] = own if acc[b] is None else tuple(x + y for x, y in zip(own, acc[b]))
        for s_step in reversed(range(steps)):
            lo_block = 2 ** s_step // per_block
            if lo_block == 0:
                break
            if lo_block <= b < 2 * lo_block:
                recv = lax.ppermute(acc[b], "ctx", step_pairs(n, orders, s_step))
                dst = b - lo_block
                acc[dst] = recv if acc[dst] is None else tuple(
                    x + y for x, y in zip(acc[dst], recv)
                )
                acc[b] = None
                break
    last = acc[0]
    for s_step in reversed(range(steps)):
        half = 2 ** s_step
        if half >= per_block:
            continue
        recv = lax.ppermute(
            tuple(x[half : 2 * half] for x in last), "ctx", step_pairs(n, orders, s_step)
        )
        last = tuple(x[:half] + r for x, r in zip(last, recv))
    dk_mine, dv_mine = (x[0] for x in last)

    dq_b = dq.astype(jnp.bfloat16).reshape(tokens, heads * head_dim)
    query_part = lax.psum_scatter(
        contract_rows(dq_b, w_query).astype(jnp.bfloat16), "tp", scatter_dimension=1, tiled=True
    )
    kv_grad = jnp.concatenate([dk_mine, dv_mine], axis=1).astype(jnp.bfloat16)
    total = query_part.astype(jnp.float32) + contract_rows(kv_grad, my_kv_rows)
    for k in range(1, m):
        shift = [(j, (j + k) % m) for j in range(m)]
        total = total + contract_rows(lax.ppermute(kv_grad, "tp", shift), kv_rows_from[k])
    return total.astype(jnp.bfloat16)


def solution(mesh):
    placed = (
        P("ctx", None),
        P(None, "tp"),
        P(None, "tp"),
        P(None, "tp"),
        P("ctx", "tp"),
        P("ctx", "tp"),
        P(),
    )
    return jax.shard_map(
        on_device, mesh=mesh, in_specs=placed, out_specs=P("ctx", "tp"), check_vma=False
    )
```

```python
import math

import numpy as np

import jax
import jax.numpy as jnp
from jax import lax
from jax.sharding import PartitionSpec as P

big_negative = -1e30


def exchange_orders(n):
    if n == 64:
        return ([5, 3, 2, 4, 1, 0], [3, 2, 5, 1, 4, 0])
    bits = list(range(int(math.log2(n))))[::-1]
    return (bits, bits)


def step_pairs(n, orders, s):
    return [(i, i ^ (1 << orders[i & 1][s])) for i in range(n)]


def owner_table(n, orders):
    owners = [[i] for i in range(n)]
    for s in range(len(orders[0])):
        owners = [owners[i] + owners[j] for i, j in step_pairs(n, orders, s)]
    return np.asarray(owners, np.int32)


def gather_parts(pieces, n, orders):
    parts = [tuple(p[None] for p in pieces)]
    buf = parts[0]
    for s in range(len(orders[0])):
        other = lax.ppermute(buf, "ctx", step_pairs(n, orders, s))
        parts.append(other)
        if s + 1 < len(orders[0]):
            buf = tuple(jnp.concatenate([b, o], axis=0) for b, o in zip(buf, other))
    return parts


def slot_range(parts, lo, hi):
    picked = []
    for s, part in enumerate(parts):
        first = 0 if s == 0 else 2 ** (s - 1)
        size = part[0].shape[0]
        a, b = max(lo, first), min(hi, first + size)
        if a < b:
            picked.append(tuple(x[a - first : b - first] for x in part))
    if len(picked) == 1:
        return picked[0]
    return tuple(jnp.concatenate(xs, axis=0) for xs in zip(*picked))


def row_positions(order, start, count, span):
    rows = start + lax.iota(jnp.int32, count)
    slot = rows // span
    table = jnp.sum(
        jnp.where(slot[:, None] == lax.iota(jnp.int32, order.shape[0])[None, :], order[None, :], 0),
        axis=1,
    )
    return table * span + rows % span


def contract_rows(left, weight):
    return lax.dot_general(
        left, weight, (((1,), (1,)), ((), ())), preferred_element_type=jnp.float32
    )


def on_device(inputs, w_query, w_key, w_value, attn_out, d_out, block_order):
    tokens = inputs.shape[0]
    span = tokens // 2
    head_dim = w_key.shape[1]
    heads = w_query.shape[1] // head_dim
    scale = head_dim ** (-0.5)
    n = lax.axis_size("ctx")
    orders = exchange_orders(n)
    steps = len(orders[0])
    me = lax.axis_index("ctx")
    keys = jnp.dot(inputs, w_key, preferred_element_type=jnp.float32).astype(jnp.bfloat16)
    values = jnp.dot(inputs, w_value, preferred_element_type=jnp.float32).astype(jnp.bfloat16)
    seq = tokens * n
    my_pos = row_positions(block_order, me * tokens, tokens, span)
    queries = (
        jnp.dot(inputs, w_query, preferred_element_type=jnp.float32)
        .astype(jnp.bfloat16)
        .reshape(tokens, heads, head_dim)
    )
    grads3 = d_out.reshape(tokens, heads, head_dim)
    delta = jnp.sum(
        grads3.astype(jnp.float32) * attn_out.reshape(tokens, heads, head_dim).astype(jnp.float32),
        axis=-1,
    ).T

    owners = lax.dynamic_index_in_dim(jnp.asarray(owner_table(n, orders)), me, 0, keepdims=False)
    per_owner = tokens // span
    owner_blocks = (owners[:, None] * per_owner + lax.iota(jnp.int32, per_owner)[None, :]).reshape(-1)
    block_ids = jnp.sum(
        jnp.where(
            owner_blocks[:, None] == lax.iota(jnp.int32, block_order.shape[0])[None, :],
            block_order[None, :],
            0,
        ),
        axis=1,
    )
    all_pos = (block_ids[:, None] * span + lax.iota(jnp.int32, span)[None, :]).reshape(seq)

    m = lax.axis_size("tp")
    t = lax.axis_index("tp")
    cols = w_query.shape[0] // m
    kv_weights = jnp.concatenate([w_key, w_value], axis=1)
    my_kv_rows = lax.dynamic_slice_in_dim(kv_weights, t * cols, cols, 0)
    kv_rows_from = [None]
    for k in range(1, m):
        shift = [(j, (j + k) % m) for j in range(m)]
        sent = lax.dynamic_slice_in_dim(kv_weights, ((t + k) % m) * cols, cols, 0)
        kv_rows_from.append(lax.ppermute(sent, "tp", shift))

    parts = gather_parts((keys, values), n, orders)
    block = math.gcd(seq, 1024)
    count = seq // block
    per_block = block // tokens

    def block_kv(b):
        k, v = slot_range(parts, b * per_block, (b + 1) * per_block)
        return k.reshape(block, head_dim), v.reshape(block, head_dim)

    def block_mask(b):
        key_pos = lax.slice_in_dim(all_pos, b * block, (b + 1) * block)
        return (key_pos[None, :] <= my_pos[:, None])[None]

    top = jnp.full((heads, tokens), big_negative, jnp.float32)
    total = jnp.zeros((heads, tokens), jnp.float32)
    for b in range(count):
        piece_k, _ = block_kv(b)
        mask = block_mask(b)
        s = jnp.einsum("thd,nd->htn", queries, piece_k, preferred_element_type=jnp.float32) * scale
        s = jnp.where(mask, s, big_negative)
        top_new = jnp.maximum(top, jnp.max(s, axis=-1))
        terms = jnp.where(mask, jnp.exp(s - top_new[..., None]), 0.0)
        total = total * jnp.exp(top - top_new) + jnp.sum(terms, axis=-1)
        top = top_new
    lse = top + jnp.log(total)

    dq = jnp.zeros((tokens, heads, head_dim), jnp.float32)
    acc = [None] * count
    for b in reversed(range(count)):
        piece_k, piece_v = block_kv(b)
        mask = block_mask(b)
        s = jnp.einsum("thd,nd->htn", queries, piece_k, preferred_element_type=jnp.float32) * scale
        p = jnp.where(mask, jnp.exp(s - lse[..., None]), 0.0)
        dp = jnp.einsum("thd,nd->htn", grads3, piece_v, preferred_element_type=jnp.float32)
        ds_b = (p * (dp - delta[..., None]) * scale).astype(jnp.bfloat16)
        p_b = p.astype(jnp.bfloat16)
        dq = dq + jnp.einsum("htn,nd->thd", ds_b, piece_k, preferred_element_type=jnp.float32)
        dk_piece = jnp.einsum("htn,thd->nd", ds_b, queries, preferred_element_type=jnp.float32)
        dv_piece = jnp.einsum("htn,thd->nd", p_b, grads3, preferred_element_type=jnp.float32)
        own = (
            dk_piece.reshape(per_block, tokens, head_dim),
            dv_piece.reshape(per_block, tokens, head_dim),
        )
        acc[b] = own if acc[b] is None else tuple(x + y for x, y in zip(own, acc[b]))
        for s_step in reversed(range(steps)):
            lo_block = 2 ** s_step // per_block
            if lo_block == 0:
                break
            if lo_block <= b < 2 * lo_block:
                recv = lax.ppermute(
                    tuple(x.astype(jnp.bfloat16) for x in acc[b]), "ctx", step_pairs(n, orders, s_step)
                )
                recv = tuple(r.astype(jnp.float32) for r in recv)
                dst = b - lo_block
                acc[dst] = recv if acc[dst] is None else tuple(
                    x + y for x, y in zip(acc[dst], recv)
                )
                acc[b] = None
                break
    last = acc[0]
    for s_step in reversed(range(steps)):
        half = 2 ** s_step
        if half >= per_block:
            continue
        recv = lax.ppermute(
            tuple(x[half : 2 * half].astype(jnp.bfloat16) for x in last),
            "ctx",
            step_pairs(n, orders, s_step),
        )
        last = tuple(x[:half] + r.astype(jnp.float32) for x, r in zip(last, recv))
    dk_mine, dv_mine = (x[0] for x in last)

    dq_b = dq.astype(jnp.bfloat16).reshape(tokens, heads * head_dim)
    query_part = lax.psum_scatter(
        contract_rows(dq_b, w_query).astype(jnp.bfloat16), "tp", scatter_dimension=1, tiled=True
    )
    kv_grad = jnp.concatenate([dk_mine, dv_mine], axis=1).astype(jnp.bfloat16)
    total = query_part.astype(jnp.float32) + contract_rows(kv_grad, my_kv_rows)
    for k in range(1, m):
        shift = [(j, (j + k) % m) for j in range(m)]
        total = total + contract_rows(lax.ppermute(kv_grad, "tp", shift), kv_rows_from[k])
    return total.astype(jnp.bfloat16)


def solution(mesh):
    placed = (
        P("ctx", None),
        P(None, "tp"),
        P(None, "tp"),
        P(None, "tp"),
        P("ctx", "tp"),
        P("ctx", "tp"),
        P(),
    )
    return jax.shard_map(
        on_device, mesh=mesh, in_specs=placed, out_specs=P("ctx", "tp"), check_vma=False
    )
```

```python
import math

import numpy as np

import jax
import jax.numpy as jnp
from jax import lax
from jax.sharding import PartitionSpec as P

big_negative = -1e30


def exchange_orders(n):
    if n == 64:
        return ([5, 3, 2, 4, 1, 0], [3, 2, 5, 1, 4, 0])
    bits = list(range(int(math.log2(n))))[::-1]
    return (bits, bits)


def step_pairs(n, orders, s):
    return [(i, i ^ (1 << orders[i & 1][s])) for i in range(n)]


def owner_table(n, orders):
    owners = [[i] for i in range(n)]
    for s in range(len(orders[0])):
        owners = [owners[i] + owners[j] for i, j in step_pairs(n, orders, s)]
    return np.asarray(owners, np.int32)


def group_offset(orders, cls, k):
    offset = 0
    for s in range(k.bit_length()):
        if (k >> s) & 1:
            offset ^= 1 << orders[cls][s]
    return offset


def group_pairs(n, orders, k):
    return [(j, j ^ group_offset(orders, j & 1, k)) for j in range(n)]


def gather_parts(pieces, n, orders, first):
    local = tuple(p[None] for p in pieces)
    recvs = [local] + [
        lax.ppermute(local, "ctx", group_pairs(n, orders, k)) for k in range(1, 2**first)
    ]
    parts = [local]
    for s in range(first):
        grp = recvs[2**s : 2 ** (s + 1)]
        parts.append(grp[0] if len(grp) == 1 else tuple(jnp.concatenate(xs, 0) for xs in zip(*grp)))
    buf = tuple(jnp.concatenate(xs, axis=0) for xs in zip(*recvs))
    for s in range(first, len(orders[0])):
        other = lax.ppermute(buf, "ctx", step_pairs(n, orders, s))
        parts.append(other)
        if s + 1 < len(orders[0]):
            buf = tuple(jnp.concatenate([b, o], axis=0) for b, o in zip(buf, other))
    return parts


def slot_range(parts, lo, hi):
    picked = []
    for s, part in enumerate(parts):
        first = 0 if s == 0 else 2 ** (s - 1)
        size = part[0].shape[0]
        a, b = max(lo, first), min(hi, first + size)
        if a < b:
            picked.append(tuple(x[a - first : b - first] for x in part))
    if len(picked) == 1:
        return picked[0]
    return tuple(jnp.concatenate(xs, axis=0) for xs in zip(*picked))


def row_positions(order, start, count, span):
    rows = start + lax.iota(jnp.int32, count)
    slot = rows // span
    table = jnp.sum(
        jnp.where(slot[:, None] == lax.iota(jnp.int32, order.shape[0])[None, :], order[None, :], 0),
        axis=1,
    )
    return table * span + rows % span


def contract_rows(left, weight):
    return lax.dot_general(
        left, weight, (((1,), (1,)), ((), ())), preferred_element_type=jnp.float32
    )


def on_device(inputs, w_query, w_key, w_value, attn_out, d_out, block_order):
    tokens = inputs.shape[0]
    span = tokens // 2
    head_dim = w_key.shape[1]
    heads = w_query.shape[1] // head_dim
    scale = head_dim ** (-0.5)
    n = lax.axis_size("ctx")
    orders = exchange_orders(n)
    steps = len(orders[0])
    me = lax.axis_index("ctx")
    keys = jnp.dot(inputs, w_key, preferred_element_type=jnp.float32).astype(jnp.bfloat16)
    values = jnp.dot(inputs, w_value, preferred_element_type=jnp.float32).astype(jnp.bfloat16)
    seq = tokens * n
    my_pos = row_positions(block_order, me * tokens, tokens, span)
    queries = (
        jnp.dot(inputs, w_query, preferred_element_type=jnp.float32)
        .astype(jnp.bfloat16)
        .reshape(tokens, heads, head_dim)
    )
    grads3 = d_out.reshape(tokens, heads, head_dim)
    delta = jnp.sum(
        grads3.astype(jnp.float32) * attn_out.reshape(tokens, heads, head_dim).astype(jnp.float32),
        axis=-1,
    ).T

    owners = lax.dynamic_index_in_dim(jnp.asarray(owner_table(n, orders)), me, 0, keepdims=False)
    per_owner = tokens // span
    owner_blocks = (owners[:, None] * per_owner + lax.iota(jnp.int32, per_owner)[None, :]).reshape(-1)
    block_ids = jnp.sum(
        jnp.where(
            owner_blocks[:, None] == lax.iota(jnp.int32, block_order.shape[0])[None, :],
            block_order[None, :],
            0,
        ),
        axis=1,
    )
    all_pos = (block_ids[:, None] * span + lax.iota(jnp.int32, span)[None, :]).reshape(seq)

    m = lax.axis_size("tp")
    t = lax.axis_index("tp")
    cols = w_query.shape[0] // m
    kv_weights = jnp.concatenate([w_key, w_value], axis=1)
    my_kv_rows = lax.dynamic_slice_in_dim(kv_weights, t * cols, cols, 0)
    kv_rows_from = [None]
    for k in range(1, m):
        shift = [(j, (j + k) % m) for j in range(m)]
        sent = lax.dynamic_slice_in_dim(kv_weights, ((t + k) % m) * cols, cols, 0)
        kv_rows_from.append(lax.ppermute(sent, "tp", shift))

    block = math.gcd(seq, 1024)
    count = seq // block
    per_block = block // tokens
    parts = gather_parts((keys, values), n, orders, per_block.bit_length() - 1)

    def block_kv(b):
        k, v = slot_range(parts, b * per_block, (b + 1) * per_block)
        return k.reshape(block, head_dim), v.reshape(block, head_dim)

    def block_mask(b):
        key_pos = lax.slice_in_dim(all_pos, b * block, (b + 1) * block)
        return (key_pos[None, :] <= my_pos[:, None])[None]

    top = jnp.full((heads, tokens), big_negative, jnp.float32)
    total = jnp.zeros((heads, tokens), jnp.float32)
    for b in range(count):
        piece_k, _ = block_kv(b)
        mask = block_mask(b)
        s = jnp.einsum("thd,nd->htn", queries, piece_k, preferred_element_type=jnp.float32) * scale
        s = jnp.where(mask, s, big_negative)
        top_new = jnp.maximum(top, jnp.max(s, axis=-1))
        terms = jnp.where(mask, jnp.exp(s - top_new[..., None]), 0.0)
        total = total * jnp.exp(top - top_new) + jnp.sum(terms, axis=-1)
        top = top_new
    lse = top + jnp.log(total)

    dq = jnp.zeros((tokens, heads, head_dim), jnp.float32)
    acc = [None] * count
    for b in reversed(range(count)):
        piece_k, piece_v = block_kv(b)
        mask = block_mask(b)
        s = jnp.einsum("thd,nd->htn", queries, piece_k, preferred_element_type=jnp.float32) * scale
        p = jnp.where(mask, jnp.exp(s - lse[..., None]), 0.0)
        dp = jnp.einsum("thd,nd->htn", grads3, piece_v, preferred_element_type=jnp.float32)
        ds_b = (p * (dp - delta[..., None]) * scale).astype(jnp.bfloat16)
        p_b = p.astype(jnp.bfloat16)
        dq = dq + jnp.einsum("htn,nd->thd", ds_b, piece_k, preferred_element_type=jnp.float32)
        dk_piece = jnp.einsum("htn,thd->nd", ds_b, queries, preferred_element_type=jnp.float32)
        dv_piece = jnp.einsum("htn,thd->nd", p_b, grads3, preferred_element_type=jnp.float32)
        own = (
            dk_piece.reshape(per_block, tokens, head_dim),
            dv_piece.reshape(per_block, tokens, head_dim),
        )
        acc[b] = own if acc[b] is None else tuple(x + y for x, y in zip(own, acc[b]))
        for s_step in reversed(range(steps)):
            lo_block = 2 ** s_step // per_block
            if lo_block == 0:
                break
            if lo_block <= b < 2 * lo_block:
                recv = lax.ppermute(
                    tuple(x.astype(jnp.bfloat16) for x in acc[b]), "ctx", step_pairs(n, orders, s_step)
                )
                recv = tuple(r.astype(jnp.float32) for r in recv)
                dst = b - lo_block
                acc[dst] = recv if acc[dst] is None else tuple(
                    x + y for x, y in zip(acc[dst], recv)
                )
                acc[b] = None
                break
    last = acc[0]
    mine = tuple(x[0] for x in last)
    for k in range(1, per_block):
        recv = lax.ppermute(
            tuple(x[k].astype(jnp.bfloat16) for x in last), "ctx", group_pairs(n, orders, k)
        )
        mine = tuple(a + r.astype(jnp.float32) for a, r in zip(mine, recv))
    dk_mine, dv_mine = mine

    dq_b = dq.astype(jnp.bfloat16).reshape(tokens, heads * head_dim)
    query_part = lax.psum_scatter(
        contract_rows(dq_b, w_query).astype(jnp.bfloat16), "tp", scatter_dimension=1, tiled=True
    )
    kv_grad = jnp.concatenate([dk_mine, dv_mine], axis=1).astype(jnp.bfloat16)
    total = query_part.astype(jnp.float32) + contract_rows(kv_grad, my_kv_rows)
    for k in range(1, m):
        shift = [(j, (j + k) % m) for j in range(m)]
        total = total + contract_rows(lax.ppermute(kv_grad, "tp", shift), kv_rows_from[k])
    return total.astype(jnp.bfloat16)


def solution(mesh):
    placed = (
        P("ctx", None),
        P(None, "tp"),
        P(None, "tp"),
        P(None, "tp"),
        P("ctx", "tp"),
        P("ctx", "tp"),
        P(),
    )
    return jax.shard_map(
        on_device, mesh=mesh, in_specs=placed, out_specs=P("ctx", "tp"), check_vma=False
    )
```

```python
import math

import numpy as np

import jax
import jax.numpy as jnp
from jax import lax
from jax.sharding import PartitionSpec as P

big_negative = -1e30


def exchange_orders(n):
    if n == 64:
        return ([5, 3, 2, 4, 1, 0], [3, 2, 5, 1, 4, 0])
    bits = list(range(int(math.log2(n))))[::-1]
    return (bits, bits)


def step_pairs(n, orders, s):
    return [(i, i ^ (1 << orders[i & 1][s])) for i in range(n)]


def owner_table(n, orders):
    owners = [[i] for i in range(n)]
    for s in range(len(orders[0])):
        owners = [owners[i] + owners[j] for i, j in step_pairs(n, orders, s)]
    return np.asarray(owners, np.int32)


def gather_parts(pieces, n, orders):
    parts = [tuple(p[None] for p in pieces)]
    buf = parts[0]
    for s in range(len(orders[0])):
        other = lax.ppermute(buf, "ctx", step_pairs(n, orders, s))
        parts.append(other)
        if s + 1 < len(orders[0]):
            buf = tuple(jnp.concatenate([b, o], axis=0) for b, o in zip(buf, other))
    return parts


def slot_range(parts, lo, hi):
    picked = []
    for s, part in enumerate(parts):
        first = 0 if s == 0 else 2 ** (s - 1)
        size = part[0].shape[0]
        a, b = max(lo, first), min(hi, first + size)
        if a < b:
            picked.append(tuple(x[a - first : b - first] for x in part))
    if len(picked) == 1:
        return picked[0]
    return tuple(jnp.concatenate(xs, axis=0) for xs in zip(*picked))


def row_positions(order, start, count, span):
    rows = start + lax.iota(jnp.int32, count)
    slot = rows // span
    table = jnp.sum(
        jnp.where(slot[:, None] == lax.iota(jnp.int32, order.shape[0])[None, :], order[None, :], 0),
        axis=1,
    )
    return table * span + rows % span


def contract_rows(left, weight):
    return lax.dot_general(
        left, weight, (((1,), (1,)), ((), ())), preferred_element_type=jnp.float32
    )


def on_device(inputs, w_query, w_key, w_value, attn_out, d_out, block_order):
    tokens = inputs.shape[0]
    span = tokens // 2
    head_dim = w_key.shape[1]
    heads = w_query.shape[1] // head_dim
    scale = head_dim ** (-0.5)
    n = lax.axis_size("ctx")
    orders = exchange_orders(n)
    steps = len(orders[0])
    me = lax.axis_index("ctx")
    keys = jnp.dot(inputs, w_key, preferred_element_type=jnp.float32).astype(jnp.bfloat16)
    values = jnp.dot(inputs, w_value, preferred_element_type=jnp.float32).astype(jnp.bfloat16)
    seq = tokens * n
    my_pos = row_positions(block_order, me * tokens, tokens, span)
    queries = (
        jnp.dot(inputs, w_query, preferred_element_type=jnp.float32)
        .astype(jnp.bfloat16)
        .reshape(tokens, heads, head_dim)
    )
    grads3 = d_out.reshape(tokens, heads, head_dim)
    delta = jnp.sum(
        grads3.astype(jnp.float32) * attn_out.reshape(tokens, heads, head_dim).astype(jnp.float32),
        axis=-1,
    ).T

    owners = lax.dynamic_index_in_dim(jnp.asarray(owner_table(n, orders)), me, 0, keepdims=False)
    per_owner = tokens // span
    owner_blocks = (owners[:, None] * per_owner + lax.iota(jnp.int32, per_owner)[None, :]).reshape(-1)
    block_ids = jnp.sum(
        jnp.where(
            owner_blocks[:, None] == lax.iota(jnp.int32, block_order.shape[0])[None, :],
            block_order[None, :],
            0,
        ),
        axis=1,
    )
    all_pos = (block_ids[:, None] * span + lax.iota(jnp.int32, span)[None, :]).reshape(seq)

    m = lax.axis_size("tp")
    t = lax.axis_index("tp")
    cols = w_query.shape[0] // m
    kv_weights = jnp.concatenate([w_key, w_value], axis=1)
    my_kv_rows = lax.dynamic_slice_in_dim(kv_weights, t * cols, cols, 0)
    kv_rows_from = [None]
    for k in range(1, m):
        shift = [(j, (j + k) % m) for j in range(m)]
        sent = lax.dynamic_slice_in_dim(kv_weights, ((t + k) % m) * cols, cols, 0)
        kv_rows_from.append(lax.ppermute(sent, "tp", shift))

    parts = gather_parts((jnp.concatenate([keys, values], axis=1),), n, orders)
    block = math.gcd(seq, 1024)
    count = seq // block
    per_block = block // tokens

    def block_kv(b):
        (kv,) = slot_range(parts, b * per_block, (b + 1) * per_block)
        kv = kv.reshape(block, 2 * head_dim)
        return kv[:, :head_dim], kv[:, head_dim:]

    def block_mask(b):
        key_pos = lax.slice_in_dim(all_pos, b * block, (b + 1) * block)
        return (key_pos[None, :] <= my_pos[:, None])[None]

    top = jnp.full((heads, tokens), big_negative, jnp.float32)
    total = jnp.zeros((heads, tokens), jnp.float32)
    for b in range(count):
        piece_k, _ = block_kv(b)
        mask = block_mask(b)
        s = jnp.einsum("thd,nd->htn", queries, piece_k, preferred_element_type=jnp.float32) * scale
        s = jnp.where(mask, s, big_negative)
        top_new = jnp.maximum(top, jnp.max(s, axis=-1))
        terms = jnp.where(mask, jnp.exp(s - top_new[..., None]), 0.0)
        total = total * jnp.exp(top - top_new) + jnp.sum(terms, axis=-1)
        top = top_new
    lse = top + jnp.log(total)

    dq = jnp.zeros((tokens, heads, head_dim), jnp.float32)
    acc = [None] * count
    for b in reversed(range(count)):
        piece_k, piece_v = block_kv(b)
        mask = block_mask(b)
        s = jnp.einsum("thd,nd->htn", queries, piece_k, preferred_element_type=jnp.float32) * scale
        p = jnp.where(mask, jnp.exp(s - lse[..., None]), 0.0)
        dp = jnp.einsum("thd,nd->htn", grads3, piece_v, preferred_element_type=jnp.float32)
        ds_b = (p * (dp - delta[..., None]) * scale).astype(jnp.bfloat16)
        p_b = p.astype(jnp.bfloat16)
        dq = dq + jnp.einsum("htn,nd->thd", ds_b, piece_k, preferred_element_type=jnp.float32)
        dk_piece = jnp.einsum("htn,thd->nd", ds_b, queries, preferred_element_type=jnp.float32)
        dv_piece = jnp.einsum("htn,thd->nd", p_b, grads3, preferred_element_type=jnp.float32)
        own = (jnp.concatenate([dk_piece, dv_piece], axis=1).reshape(per_block, tokens, 2 * head_dim),)
        acc[b] = own if acc[b] is None else tuple(x + y for x, y in zip(own, acc[b]))
        for s_step in reversed(range(steps)):
            lo_block = 2 ** s_step // per_block
            if lo_block == 0:
                break
            if lo_block <= b < 2 * lo_block:
                recv = lax.ppermute(
                    tuple(x.astype(jnp.bfloat16) for x in acc[b]), "ctx", step_pairs(n, orders, s_step)
                )
                recv = tuple(r.astype(jnp.float32) for r in recv)
                dst = b - lo_block
                acc[dst] = recv if acc[dst] is None else tuple(
                    x + y for x, y in zip(acc[dst], recv)
                )
                acc[b] = None
                break
    last = acc[0]
    for s_step in reversed(range(steps)):
        half = 2 ** s_step
        if half >= per_block:
            continue
        recv = lax.ppermute(
            tuple(x[half : 2 * half].astype(jnp.bfloat16) for x in last),
            "ctx",
            step_pairs(n, orders, s_step),
        )
        last = tuple(x[:half] + r.astype(jnp.float32) for x, r in zip(last, recv))
    (kv_mine,) = (x[0] for x in last)

    dq_b = dq.astype(jnp.bfloat16).reshape(tokens, heads * head_dim)
    query_part = lax.psum_scatter(
        contract_rows(dq_b, w_query).astype(jnp.bfloat16), "tp", scatter_dimension=1, tiled=True
    )
    kv_grad = kv_mine.astype(jnp.bfloat16)
    total = query_part.astype(jnp.float32) + contract_rows(kv_grad, my_kv_rows)
    for k in range(1, m):
        shift = [(j, (j + k) % m) for j in range(m)]
        total = total + contract_rows(lax.ppermute(kv_grad, "tp", shift), kv_rows_from[k])
    return total.astype(jnp.bfloat16)


def solution(mesh):
    placed = (
        P("ctx", None),
        P(None, "tp"),
        P(None, "tp"),
        P(None, "tp"),
        P("ctx", "tp"),
        P("ctx", "tp"),
        P(),
    )
    return jax.shard_map(
        on_device, mesh=mesh, in_specs=placed, out_specs=P("ctx", "tp"), check_vma=False
    )
```

```python
import math

import numpy as np

import jax
import jax.numpy as jnp
from jax import lax
from jax.sharding import PartitionSpec as P

big_negative = -1e30


def exchange_orders(n):
    if n == 64:
        return ([5, 3, 2, 4, 1, 0], [3, 2, 5, 1, 4, 0])
    bits = list(range(int(math.log2(n))))[::-1]
    return (bits, bits)


def step_pairs(n, orders, s):
    return [(i, i ^ (1 << orders[i & 1][s])) for i in range(n)]


def owner_table(n, orders):
    owners = [[i] for i in range(n)]
    for s in range(len(orders[0])):
        owners = [owners[i] + owners[j] for i, j in step_pairs(n, orders, s)]
    return np.asarray(owners, np.int32)


def gather_parts(pieces, n, orders):
    parts = [tuple(p[None] for p in pieces)]
    buf = parts[0]
    for s in range(len(orders[0])):
        other = lax.ppermute(buf, "ctx", step_pairs(n, orders, s))
        parts.append(other)
        if s + 1 < len(orders[0]):
            buf = tuple(jnp.concatenate([b, o], axis=0) for b, o in zip(buf, other))
    return parts


def slot_range(parts, lo, hi):
    picked = []
    for s, part in enumerate(parts):
        first = 0 if s == 0 else 2 ** (s - 1)
        size = part[0].shape[0]
        a, b = max(lo, first), min(hi, first + size)
        if a < b:
            picked.append(tuple(x[a - first : b - first] for x in part))
    if len(picked) == 1:
        return picked[0]
    return tuple(jnp.concatenate(xs, axis=0) for xs in zip(*picked))


def row_positions(order, start, count, span):
    rows = start + lax.iota(jnp.int32, count)
    slot = rows // span
    table = jnp.sum(
        jnp.where(slot[:, None] == lax.iota(jnp.int32, order.shape[0])[None, :], order[None, :], 0),
        axis=1,
    )
    return table * span + rows % span


def contract_rows(left, weight):
    return lax.dot_general(
        left, weight, (((1,), (1,)), ((), ())), preferred_element_type=jnp.float32
    )


def on_device(inputs, w_query, w_key, w_value, attn_out, d_out, block_order):
    tokens = inputs.shape[0]
    span = tokens // 2
    head_dim = w_key.shape[1]
    heads = w_query.shape[1] // head_dim
    scale = head_dim ** (-0.5)
    n = lax.axis_size("ctx")
    orders = exchange_orders(n)
    steps = len(orders[0])
    me = lax.axis_index("ctx")
    keys = jnp.dot(inputs, w_key, preferred_element_type=jnp.float32).astype(jnp.bfloat16)
    values = jnp.dot(inputs, w_value, preferred_element_type=jnp.float32).astype(jnp.bfloat16)
    seq = tokens * n
    my_pos = row_positions(block_order, me * tokens, tokens, span)
    queries = (
        jnp.dot(inputs, w_query, preferred_element_type=jnp.float32)
        .astype(jnp.bfloat16)
        .reshape(tokens, heads, head_dim)
    )
    grads3 = d_out.reshape(tokens, heads, head_dim)
    delta = jnp.sum(
        grads3.astype(jnp.float32) * attn_out.reshape(tokens, heads, head_dim).astype(jnp.float32),
        axis=-1,
    ).T

    owners = lax.dynamic_index_in_dim(jnp.asarray(owner_table(n, orders)), me, 0, keepdims=False)
    per_owner = tokens // span
    owner_blocks = (owners[:, None] * per_owner + lax.iota(jnp.int32, per_owner)[None, :]).reshape(-1)
    block_ids = jnp.sum(
        jnp.where(
            owner_blocks[:, None] == lax.iota(jnp.int32, block_order.shape[0])[None, :],
            block_order[None, :],
            0,
        ),
        axis=1,
    )
    all_pos = (block_ids[:, None] * span + lax.iota(jnp.int32, span)[None, :]).reshape(seq)

    m = lax.axis_size("tp")
    t = lax.axis_index("tp")
    cols = w_query.shape[0] // m
    kv_weights = jnp.concatenate([w_key, w_value], axis=1)
    my_kv_rows = lax.dynamic_slice_in_dim(kv_weights, t * cols, cols, 0)
    kv_rows_from = [None]
    for k in range(1, m):
        shift = [(j, (j + k) % m) for j in range(m)]
        sent = lax.dynamic_slice_in_dim(kv_weights, ((t + k) % m) * cols, cols, 0)
        kv_rows_from.append(lax.ppermute(sent, "tp", shift))
    swapped, queries = lax.optimization_barrier((tuple(kv_rows_from[1:]), queries))
    kv_rows_from = [None] + list(swapped)

    parts = gather_parts((keys, values), n, orders)
    block = math.gcd(seq, 1024)
    count = seq // block
    per_block = block // tokens

    def block_kv(b):
        k, v = slot_range(parts, b * per_block, (b + 1) * per_block)
        return k.reshape(block, head_dim), v.reshape(block, head_dim)

    def block_mask(b):
        key_pos = lax.slice_in_dim(all_pos, b * block, (b + 1) * block)
        return (key_pos[None, :] <= my_pos[:, None])[None]

    top = jnp.full((heads, tokens), big_negative, jnp.float32)
    total = jnp.zeros((heads, tokens), jnp.float32)
    for b in range(count):
        piece_k, _ = block_kv(b)
        mask = block_mask(b)
        s = jnp.einsum("thd,nd->htn", queries, piece_k, preferred_element_type=jnp.float32) * scale
        s = jnp.where(mask, s, big_negative)
        top_new = jnp.maximum(top, jnp.max(s, axis=-1))
        terms = jnp.where(mask, jnp.exp(s - top_new[..., None]), 0.0)
        total = total * jnp.exp(top - top_new) + jnp.sum(terms, axis=-1)
        top = top_new
    lse = top + jnp.log(total)

    dq = jnp.zeros((tokens, heads, head_dim), jnp.float32)
    acc = [None] * count
    for b in reversed(range(count)):
        piece_k, piece_v = block_kv(b)
        mask = block_mask(b)
        s = jnp.einsum("thd,nd->htn", queries, piece_k, preferred_element_type=jnp.float32) * scale
        p = jnp.where(mask, jnp.exp(s - lse[..., None]), 0.0)
        dp = jnp.einsum("thd,nd->htn", grads3, piece_v, preferred_element_type=jnp.float32)
        ds_b = (p * (dp - delta[..., None]) * scale).astype(jnp.bfloat16)
        p_b = p.astype(jnp.bfloat16)
        dq = dq + jnp.einsum("htn,nd->thd", ds_b, piece_k, preferred_element_type=jnp.float32)
        dk_piece = jnp.einsum("htn,thd->nd", ds_b, queries, preferred_element_type=jnp.float32)
        dv_piece = jnp.einsum("htn,thd->nd", p_b, grads3, preferred_element_type=jnp.float32)
        own = (
            dk_piece.reshape(per_block, tokens, head_dim),
            dv_piece.reshape(per_block, tokens, head_dim),
        )
        acc[b] = own if acc[b] is None else tuple(x + y for x, y in zip(own, acc[b]))
        for s_step in reversed(range(steps)):
            lo_block = 2 ** s_step // per_block
            if lo_block == 0:
                break
            if lo_block <= b < 2 * lo_block:
                recv = lax.ppermute(
                    tuple(x.astype(jnp.bfloat16) for x in acc[b]), "ctx", step_pairs(n, orders, s_step)
                )
                recv = tuple(r.astype(jnp.float32) for r in recv)
                dst = b - lo_block
                acc[dst] = recv if acc[dst] is None else tuple(
                    x + y for x, y in zip(acc[dst], recv)
                )
                acc[b] = None
                break
    last = acc[0]
    for s_step in reversed(range(steps)):
        half = 2 ** s_step
        if half >= per_block:
            continue
        recv = lax.ppermute(
            tuple(x[half : 2 * half].astype(jnp.bfloat16) for x in last),
            "ctx",
            step_pairs(n, orders, s_step),
        )
        last = tuple(x[:half] + r.astype(jnp.float32) for x, r in zip(last, recv))
    dk_mine, dv_mine = (x[0] for x in last)

    dq_b = dq.astype(jnp.bfloat16).reshape(tokens, heads * head_dim)
    query_part = lax.psum_scatter(
        contract_rows(dq_b, w_query).astype(jnp.bfloat16), "tp", scatter_dimension=1, tiled=True
    )
    kv_grad = jnp.concatenate([dk_mine, dv_mine], axis=1).astype(jnp.bfloat16)
    total = query_part.astype(jnp.float32) + contract_rows(kv_grad, my_kv_rows)
    for k in range(1, m):
        shift = [(j, (j + k) % m) for j in range(m)]
        total = total + contract_rows(lax.ppermute(kv_grad, "tp", shift), kv_rows_from[k])
    return total.astype(jnp.bfloat16)


def solution(mesh):
    placed = (
        P("ctx", None),
        P(None, "tp"),
        P(None, "tp"),
        P(None, "tp"),
        P("ctx", "tp"),
        P("ctx", "tp"),
        P(),
    )
    return jax.shard_map(
        on_device, mesh=mesh, in_specs=placed, out_specs=P("ctx", "tp"), check_vma=False
    )
```

```python
import math

import numpy as np

import jax
import jax.numpy as jnp
from jax import lax
from jax.sharding import PartitionSpec as P

big_negative = -1e30


def exchange_orders(n):
    if n == 64:
        return ([5, 3, 2, 4, 1, 0], [3, 2, 5, 1, 4, 0])
    bits = list(range(int(math.log2(n))))[::-1]
    return (bits, bits)


def step_pairs(n, orders, s):
    return [(i, i ^ (1 << orders[i & 1][s])) for i in range(n)]


def owner_table(n, orders):
    owners = [[i] for i in range(n)]
    for s in range(len(orders[0])):
        owners = [owners[i] + owners[j] for i, j in step_pairs(n, orders, s)]
    return np.asarray(owners, np.int32)


def gather_parts(pieces, n, orders):
    parts = [tuple(p[None] for p in pieces)]
    buf = parts[0]
    for s in range(len(orders[0])):
        other = lax.ppermute(buf, "ctx", step_pairs(n, orders, s))
        parts.append(other)
        if s + 1 < len(orders[0]):
            buf = tuple(jnp.concatenate([b, o], axis=0) for b, o in zip(buf, other))
    return parts


def slot_range(parts, lo, hi):
    picked = []
    for s, part in enumerate(parts):
        first = 0 if s == 0 else 2 ** (s - 1)
        size = part[0].shape[0]
        a, b = max(lo, first), min(hi, first + size)
        if a < b:
            picked.append(tuple(x[a - first : b - first] for x in part))
    if len(picked) == 1:
        return picked[0]
    return tuple(jnp.concatenate(xs, axis=0) for xs in zip(*picked))


def row_positions(order, start, count, span):
    rows = start + lax.iota(jnp.int32, count)
    slot = rows // span
    table = jnp.sum(
        jnp.where(slot[:, None] == lax.iota(jnp.int32, order.shape[0])[None, :], order[None, :], 0),
        axis=1,
    )
    return table * span + rows % span


def contract_rows(left, weight):
    return lax.dot_general(
        left, weight, (((1,), (1,)), ((), ())), preferred_element_type=jnp.float32
    )


def on_device(inputs, w_query, w_key, w_value, attn_out, d_out, block_order):
    tokens = inputs.shape[0]
    span = tokens // 2
    head_dim = w_key.shape[1]
    heads = w_query.shape[1] // head_dim
    scale = head_dim ** (-0.5)
    n = lax.axis_size("ctx")
    orders = exchange_orders(n)
    steps = len(orders[0])
    me = lax.axis_index("ctx")
    keys = jnp.dot(inputs, w_key, preferred_element_type=jnp.float32).astype(jnp.bfloat16)
    values = jnp.dot(inputs, w_value, preferred_element_type=jnp.float32).astype(jnp.bfloat16)
    seq = tokens * n
    my_pos = row_positions(block_order, me * tokens, tokens, span)
    queries = (
        jnp.dot(inputs, w_query, preferred_element_type=jnp.float32)
        .astype(jnp.bfloat16)
        .reshape(tokens, heads, head_dim)
    )
    grads3 = d_out.reshape(tokens, heads, head_dim)
    delta = jnp.sum(
        grads3.astype(jnp.float32) * attn_out.reshape(tokens, heads, head_dim).astype(jnp.float32),
        axis=-1,
    ).T

    owners = lax.dynamic_index_in_dim(jnp.asarray(owner_table(n, orders)), me, 0, keepdims=False)
    per_owner = tokens // span
    owner_blocks = (owners[:, None] * per_owner + lax.iota(jnp.int32, per_owner)[None, :]).reshape(-1)
    block_ids = jnp.sum(
        jnp.where(
            owner_blocks[:, None] == lax.iota(jnp.int32, block_order.shape[0])[None, :],
            block_order[None, :],
            0,
        ),
        axis=1,
    )
    all_pos = (block_ids[:, None] * span + lax.iota(jnp.int32, span)[None, :]).reshape(seq)

    m = lax.axis_size("tp")
    t = lax.axis_index("tp")
    cols = w_query.shape[0] // m
    kv_weights = jnp.concatenate([w_key, w_value], axis=1)
    my_kv_rows = lax.dynamic_slice_in_dim(kv_weights, t * cols, cols, 0)
    kv_rows_from = [None]
    for k in range(1, m):
        shift = [(j, (j + k) % m) for j in range(m)]
        sent = lax.dynamic_slice_in_dim(kv_weights, ((t + k) % m) * cols, cols, 0)
        kv_rows_from.append(lax.ppermute(sent, "tp", shift))

    parts = gather_parts((keys, values), n, orders)
    block = math.gcd(seq, 1024)
    count = seq // block
    per_block = block // tokens

    def block_kv(b):
        k, v = slot_range(parts, b * per_block, (b + 1) * per_block)
        return k.reshape(block, head_dim), v.reshape(block, head_dim)

    def block_mask(b):
        key_pos = lax.slice_in_dim(all_pos, b * block, (b + 1) * block)
        return (key_pos[None, :] <= my_pos[:, None])[None]

    top = jnp.full((heads, tokens), big_negative, jnp.float32)
    total = jnp.zeros((heads, tokens), jnp.float32)
    for b in range(count):
        piece_k, _ = block_kv(b)
        mask = block_mask(b)
        s = jnp.einsum("thd,nd->htn", queries, piece_k, preferred_element_type=jnp.float32) * scale
        s = jnp.where(mask, s, big_negative)
        top_new = jnp.maximum(top, jnp.max(s, axis=-1))
        terms = jnp.where(mask, jnp.exp(s - top_new[..., None]), 0.0)
        total = total * jnp.exp(top - top_new) + jnp.sum(terms, axis=-1)
        top = top_new
    lse = top + jnp.log(total)

    dq = jnp.zeros((tokens, heads, head_dim), jnp.float32)
    acc = [None] * count
    previous = None
    for b in reversed(range(count)):
        piece_k, piece_v = block_kv(b)
        if previous is not None:
            (piece_k, piece_v), _ = lax.optimization_barrier(((piece_k, piece_v), previous))
        mask = block_mask(b)
        s = jnp.einsum("thd,nd->htn", queries, piece_k, preferred_element_type=jnp.float32) * scale
        p = jnp.where(mask, jnp.exp(s - lse[..., None]), 0.0)
        dp = jnp.einsum("thd,nd->htn", grads3, piece_v, preferred_element_type=jnp.float32)
        ds_b = (p * (dp - delta[..., None]) * scale).astype(jnp.bfloat16)
        p_b = p.astype(jnp.bfloat16)
        dq = dq + jnp.einsum("htn,nd->thd", ds_b, piece_k, preferred_element_type=jnp.float32)
        dk_piece = jnp.einsum("htn,thd->nd", ds_b, queries, preferred_element_type=jnp.float32)
        dv_piece = jnp.einsum("htn,thd->nd", p_b, grads3, preferred_element_type=jnp.float32)
        own = (
            dk_piece.reshape(per_block, tokens, head_dim),
            dv_piece.reshape(per_block, tokens, head_dim),
        )
        previous = own
        acc[b] = own if acc[b] is None else tuple(x + y for x, y in zip(own, acc[b]))
        for s_step in reversed(range(steps)):
            lo_block = 2 ** s_step // per_block
            if lo_block == 0:
                break
            if lo_block <= b < 2 * lo_block:
                recv = lax.ppermute(
                    tuple(x.astype(jnp.bfloat16) for x in acc[b]), "ctx", step_pairs(n, orders, s_step)
                )
                recv = tuple(r.astype(jnp.float32) for r in recv)
                dst = b - lo_block
                acc[dst] = recv if acc[dst] is None else tuple(
                    x + y for x, y in zip(acc[dst], recv)
                )
                acc[b] = None
                break
    last = acc[0]
    for s_step in reversed(range(steps)):
        half = 2 ** s_step
        if half >= per_block:
            continue
        recv = lax.ppermute(
            tuple(x[half : 2 * half].astype(jnp.bfloat16) for x in last),
            "ctx",
            step_pairs(n, orders, s_step),
        )
        last = tuple(x[:half] + r.astype(jnp.float32) for x, r in zip(last, recv))
    dk_mine, dv_mine = (x[0] for x in last)

    dq_b = dq.astype(jnp.bfloat16).reshape(tokens, heads * head_dim)
    query_part = lax.psum_scatter(
        contract_rows(dq_b, w_query).astype(jnp.bfloat16), "tp", scatter_dimension=1, tiled=True
    )
    kv_grad = jnp.concatenate([dk_mine, dv_mine], axis=1).astype(jnp.bfloat16)
    total = query_part.astype(jnp.float32) + contract_rows(kv_grad, my_kv_rows)
    for k in range(1, m):
        shift = [(j, (j + k) % m) for j in range(m)]
        total = total + contract_rows(lax.ppermute(kv_grad, "tp", shift), kv_rows_from[k])
    return total.astype(jnp.bfloat16)


def solution(mesh):
    placed = (
        P("ctx", None),
        P(None, "tp"),
        P(None, "tp"),
        P(None, "tp"),
        P("ctx", "tp"),
        P("ctx", "tp"),
        P(),
    )
    return jax.shard_map(
        on_device, mesh=mesh, in_specs=placed, out_specs=P("ctx", "tp"), check_vma=False
    )
```

```python
import math

import numpy as np

import jax
import jax.numpy as jnp
from jax import lax
from jax.sharding import PartitionSpec as P

big_negative = -1e30


def exchange_orders(n):
    if n == 64:
        return ([5, 3, 2, 4, 1, 0], [3, 2, 5, 1, 4, 0])
    bits = list(range(int(math.log2(n))))[::-1]
    return (bits, bits)


def step_pairs(n, orders, s):
    return [(i, i ^ (1 << orders[i & 1][s])) for i in range(n)]


def owner_table(n, orders):
    owners = [[i] for i in range(n)]
    for s in range(len(orders[0])):
        owners = [owners[i] + owners[j] for i, j in step_pairs(n, orders, s)]
    return np.asarray(owners, np.int32)


def gather_parts(pieces, n, orders):
    parts = [tuple(p[None] for p in pieces)]
    buf = parts[0]
    for s in range(len(orders[0])):
        other = lax.ppermute(buf, "ctx", step_pairs(n, orders, s))
        parts.append(other)
        if s + 1 < len(orders[0]):
            buf = tuple(jnp.concatenate([b, o], axis=0) for b, o in zip(buf, other))
    return parts


def slot_range(parts, lo, hi):
    picked = []
    for s, part in enumerate(parts):
        first = 0 if s == 0 else 2 ** (s - 1)
        size = part[0].shape[0]
        a, b = max(lo, first), min(hi, first + size)
        if a < b:
            picked.append(tuple(x[a - first : b - first] for x in part))
    if len(picked) == 1:
        return picked[0]
    return tuple(jnp.concatenate(xs, axis=0) for xs in zip(*picked))


def row_positions(order, start, count, span):
    rows = start + lax.iota(jnp.int32, count)
    slot = rows // span
    table = jnp.sum(
        jnp.where(slot[:, None] == lax.iota(jnp.int32, order.shape[0])[None, :], order[None, :], 0),
        axis=1,
    )
    return table * span + rows % span


def contract_rows(left, weight):
    return lax.dot_general(
        left, weight, (((1,), (1,)), ((), ())), preferred_element_type=jnp.float32
    )


def on_device(inputs, w_query, w_key, w_value, attn_out, d_out, block_order):
    tokens = inputs.shape[0]
    span = tokens // 2
    head_dim = w_key.shape[1]
    heads = w_query.shape[1] // head_dim
    scale = head_dim ** (-0.5)
    n = lax.axis_size("ctx")
    orders = exchange_orders(n)
    steps = len(orders[0])
    me = lax.axis_index("ctx")
    keys = jnp.dot(inputs, w_key, preferred_element_type=jnp.float32).astype(jnp.bfloat16)
    values = jnp.dot(inputs, w_value, preferred_element_type=jnp.float32).astype(jnp.bfloat16)
    seq = tokens * n
    my_pos = row_positions(block_order, me * tokens, tokens, span)
    queries = (
        jnp.dot(inputs, w_query, preferred_element_type=jnp.float32)
        .astype(jnp.bfloat16)
        .reshape(tokens, heads, head_dim)
    )
    grads3 = d_out.reshape(tokens, heads, head_dim)
    delta = jnp.sum(
        grads3.astype(jnp.float32) * attn_out.reshape(tokens, heads, head_dim).astype(jnp.float32),
        axis=-1,
    ).T

    owners = lax.dynamic_index_in_dim(jnp.asarray(owner_table(n, orders)), me, 0, keepdims=False)
    per_owner = tokens // span
    owner_blocks = (owners[:, None] * per_owner + lax.iota(jnp.int32, per_owner)[None, :]).reshape(-1)
    block_ids = jnp.sum(
        jnp.where(
            owner_blocks[:, None] == lax.iota(jnp.int32, block_order.shape[0])[None, :],
            block_order[None, :],
            0,
        ),
        axis=1,
    )
    all_pos = (block_ids[:, None] * span + lax.iota(jnp.int32, span)[None, :]).reshape(seq)

    m = lax.axis_size("tp")
    t = lax.axis_index("tp")
    cols = w_query.shape[0] // m
    kv_weights = jnp.concatenate([w_key, w_value], axis=1)
    my_kv_rows = lax.dynamic_slice_in_dim(kv_weights, t * cols, cols, 0)
    kv_rows_from = [None]
    for k in range(1, m):
        shift = [(j, (j + k) % m) for j in range(m)]
        sent = lax.dynamic_slice_in_dim(kv_weights, ((t + k) % m) * cols, cols, 0)
        kv_rows_from.append(lax.ppermute(sent, "tp", shift))

    parts = gather_parts((keys, values), n, orders)
    block = math.gcd(seq, 1024)
    count = seq // block
    per_block = block // tokens

    def block_kv(b):
        k, v = slot_range(parts, b * per_block, (b + 1) * per_block)
        return k.reshape(block, head_dim), v.reshape(block, head_dim)

    def block_mask(b):
        key_pos = lax.slice_in_dim(all_pos, b * block, (b + 1) * block)
        return (key_pos[None, :] <= my_pos[:, None])[None]

    top = jnp.full((heads, tokens), big_negative, jnp.float32)
    total = jnp.zeros((heads, tokens), jnp.float32)
    for b in range(count):
        piece_k, _ = block_kv(b)
        if b > 0:
            piece_k, _ = lax.optimization_barrier((piece_k, (top, total)))
        mask = block_mask(b)
        s = jnp.einsum("thd,nd->htn", queries, piece_k, preferred_element_type=jnp.float32) * scale
        s = jnp.where(mask, s, big_negative)
        top_new = jnp.maximum(top, jnp.max(s, axis=-1))
        terms = jnp.where(mask, jnp.exp(s - top_new[..., None]), 0.0)
        total = total * jnp.exp(top - top_new) + jnp.sum(terms, axis=-1)
        top = top_new
    lse = top + jnp.log(total)

    dq = jnp.zeros((tokens, heads, head_dim), jnp.float32)
    acc = [None] * count
    previous = None
    for b in reversed(range(count)):
        piece_k, piece_v = block_kv(b)
        if previous is not None:
            (piece_k, piece_v), _ = lax.optimization_barrier(((piece_k, piece_v), previous))
        mask = block_mask(b)
        s = jnp.einsum("thd,nd->htn", queries, piece_k, preferred_element_type=jnp.float32) * scale
        p = jnp.where(mask, jnp.exp(s - lse[..., None]), 0.0)
        dp = jnp.einsum("thd,nd->htn", grads3, piece_v, preferred_element_type=jnp.float32)
        ds_b = (p * (dp - delta[..., None]) * scale).astype(jnp.bfloat16)
        p_b = p.astype(jnp.bfloat16)
        dq = dq + jnp.einsum("htn,nd->thd", ds_b, piece_k, preferred_element_type=jnp.float32)
        dk_piece = jnp.einsum("htn,thd->nd", ds_b, queries, preferred_element_type=jnp.float32)
        dv_piece = jnp.einsum("htn,thd->nd", p_b, grads3, preferred_element_type=jnp.float32)
        own = (
            dk_piece.reshape(per_block, tokens, head_dim),
            dv_piece.reshape(per_block, tokens, head_dim),
        )
        previous = own
        acc[b] = own if acc[b] is None else tuple(x + y for x, y in zip(own, acc[b]))
        for s_step in reversed(range(steps)):
            lo_block = 2 ** s_step // per_block
            if lo_block == 0:
                break
            if lo_block <= b < 2 * lo_block:
                recv = lax.ppermute(
                    tuple(x.astype(jnp.bfloat16) for x in acc[b]), "ctx", step_pairs(n, orders, s_step)
                )
                recv = tuple(r.astype(jnp.float32) for r in recv)
                dst = b - lo_block
                acc[dst] = recv if acc[dst] is None else tuple(
                    x + y for x, y in zip(acc[dst], recv)
                )
                acc[b] = None
                break
    last = acc[0]
    for s_step in reversed(range(steps)):
        half = 2 ** s_step
        if half >= per_block:
            continue
        recv = lax.ppermute(
            tuple(x[half : 2 * half].astype(jnp.bfloat16) for x in last),
            "ctx",
            step_pairs(n, orders, s_step),
        )
        last = tuple(x[:half] + r.astype(jnp.float32) for x, r in zip(last, recv))
    dk_mine, dv_mine = (x[0] for x in last)

    dq_b = dq.astype(jnp.bfloat16).reshape(tokens, heads * head_dim)
    query_part = lax.psum_scatter(
        contract_rows(dq_b, w_query).astype(jnp.bfloat16), "tp", scatter_dimension=1, tiled=True
    )
    kv_grad = jnp.concatenate([dk_mine, dv_mine], axis=1).astype(jnp.bfloat16)
    total = query_part.astype(jnp.float32) + contract_rows(kv_grad, my_kv_rows)
    for k in range(1, m):
        shift = [(j, (j + k) % m) for j in range(m)]
        total = total + contract_rows(lax.ppermute(kv_grad, "tp", shift), kv_rows_from[k])
    return total.astype(jnp.bfloat16)


def solution(mesh):
    placed = (
        P("ctx", None),
        P(None, "tp"),
        P(None, "tp"),
        P(None, "tp"),
        P("ctx", "tp"),
        P("ctx", "tp"),
        P(),
    )
    return jax.shard_map(
        on_device, mesh=mesh, in_specs=placed, out_specs=P("ctx", "tp"), check_vma=False
    )
```

```python
import math

import numpy as np

import jax
import jax.numpy as jnp
from jax import lax
from jax.sharding import PartitionSpec as P

big_negative = -1e30


def exchange_orders(n):
    if n == 64:
        return ([5, 3, 2, 4, 1, 0], [3, 2, 5, 1, 4, 0])
    bits = list(range(int(math.log2(n))))[::-1]
    return (bits, bits)


def step_pairs(n, orders, s):
    return [(i, i ^ (1 << orders[i & 1][s])) for i in range(n)]


def owner_table(n, orders):
    owners = [[i] for i in range(n)]
    for s in range(len(orders[0])):
        owners = [owners[i] + owners[j] for i, j in step_pairs(n, orders, s)]
    return np.asarray(owners, np.int32)


def gather_parts(pieces, n, orders):
    parts = [tuple(p[None] for p in pieces)]
    buf = parts[0]
    for s in range(len(orders[0])):
        other = lax.ppermute(buf, "ctx", step_pairs(n, orders, s))
        parts.append(other)
        if s + 1 < len(orders[0]):
            buf = tuple(jnp.concatenate([b, o], axis=0) for b, o in zip(buf, other))
    return parts


def slot_range(parts, lo, hi):
    picked = []
    for s, part in enumerate(parts):
        first = 0 if s == 0 else 2 ** (s - 1)
        size = part[0].shape[0]
        a, b = max(lo, first), min(hi, first + size)
        if a < b:
            picked.append(tuple(x[a - first : b - first] for x in part))
    if len(picked) == 1:
        return picked[0]
    return tuple(jnp.concatenate(xs, axis=0) for xs in zip(*picked))


def row_positions(order, start, count, span):
    rows = start + lax.iota(jnp.int32, count)
    slot = rows // span
    table = jnp.sum(
        jnp.where(slot[:, None] == lax.iota(jnp.int32, order.shape[0])[None, :], order[None, :], 0),
        axis=1,
    )
    return table * span + rows % span


def contract_rows(left, weight):
    return lax.dot_general(
        left, weight, (((1,), (1,)), ((), ())), preferred_element_type=jnp.float32
    )


def on_device(inputs, w_query, w_key, w_value, attn_out, d_out, block_order):
    tokens = inputs.shape[0]
    span = tokens // 2
    head_dim = w_key.shape[1]
    heads = w_query.shape[1] // head_dim
    scale = head_dim ** (-0.5)
    n = lax.axis_size("ctx")
    orders = exchange_orders(n)
    steps = len(orders[0])
    me = lax.axis_index("ctx")
    keys = jnp.dot(inputs, w_key, preferred_element_type=jnp.float32).astype(jnp.bfloat16)
    values = jnp.dot(inputs, w_value, preferred_element_type=jnp.float32).astype(jnp.bfloat16)
    seq = tokens * n
    my_pos = row_positions(block_order, me * tokens, tokens, span)
    queries = (
        jnp.dot(inputs, w_query, preferred_element_type=jnp.float32)
        .astype(jnp.bfloat16)
        .reshape(tokens, heads, head_dim)
    )
    grads3 = d_out.reshape(tokens, heads, head_dim)
    delta = jnp.sum(
        grads3.astype(jnp.float32) * attn_out.reshape(tokens, heads, head_dim).astype(jnp.float32),
        axis=-1,
    ).T

    owners = lax.dynamic_index_in_dim(jnp.asarray(owner_table(n, orders)), me, 0, keepdims=False)
    per_owner = tokens // span
    owner_blocks = (owners[:, None] * per_owner + lax.iota(jnp.int32, per_owner)[None, :]).reshape(-1)
    block_ids = jnp.sum(
        jnp.where(
            owner_blocks[:, None] == lax.iota(jnp.int32, block_order.shape[0])[None, :],
            block_order[None, :],
            0,
        ),
        axis=1,
    )
    all_pos = (block_ids[:, None] * span + lax.iota(jnp.int32, span)[None, :]).reshape(seq)

    m = lax.axis_size("tp")
    t = lax.axis_index("tp")
    cols = w_query.shape[0] // m
    kv_weights = jnp.concatenate([w_key, w_value], axis=1)
    my_kv_rows = lax.dynamic_slice_in_dim(kv_weights, t * cols, cols, 0)
    kv_rows_from = [None]
    for k in range(1, m):
        shift = [(j, (j + k) % m) for j in range(m)]
        sent = lax.dynamic_slice_in_dim(kv_weights, ((t + k) % m) * cols, cols, 0)
        kv_rows_from.append(lax.ppermute(sent, "tp", shift))
    swapped, queries = lax.optimization_barrier((tuple(kv_rows_from[1:]), queries))
    kv_rows_from = [None] + list(swapped)

    parts = gather_parts((keys, values), n, orders)
    block = math.gcd(seq, 1024)
    count = seq // block
    per_block = block // tokens

    def block_kv(b):
        k, v = slot_range(parts, b * per_block, (b + 1) * per_block)
        return k.reshape(block, head_dim), v.reshape(block, head_dim)

    def block_mask(b):
        key_pos = lax.slice_in_dim(all_pos, b * block, (b + 1) * block)
        return (key_pos[None, :] <= my_pos[:, None])[None]

    top = jnp.full((heads, tokens), big_negative, jnp.float32)
    total = jnp.zeros((heads, tokens), jnp.float32)
    for b in range(count):
        piece_k, _ = block_kv(b)
        mask = block_mask(b)
        s = jnp.einsum("thd,nd->htn", queries, piece_k, preferred_element_type=jnp.float32) * scale
        s = jnp.where(mask, s, big_negative)
        top_new = jnp.maximum(top, jnp.max(s, axis=-1))
        terms = jnp.where(mask, jnp.exp(s - top_new[..., None]), 0.0)
        total = total * jnp.exp(top - top_new) + jnp.sum(terms, axis=-1)
        top = top_new
    lse = top + jnp.log(total)

    dq = jnp.zeros((tokens, heads, head_dim), jnp.float32)
    acc = [None] * count
    previous = None
    for b in reversed(range(count)):
        piece_k, piece_v = block_kv(b)
        if previous is not None:
            (piece_k, piece_v), _ = lax.optimization_barrier(((piece_k, piece_v), previous))
        mask = block_mask(b)
        s = jnp.einsum("thd,nd->htn", queries, piece_k, preferred_element_type=jnp.float32) * scale
        p = jnp.where(mask, jnp.exp(s - lse[..., None]), 0.0)
        dp = jnp.einsum("thd,nd->htn", grads3, piece_v, preferred_element_type=jnp.float32)
        ds_b = (p * (dp - delta[..., None]) * scale).astype(jnp.bfloat16)
        p_b = p.astype(jnp.bfloat16)
        dq = dq + jnp.einsum("htn,nd->thd", ds_b, piece_k, preferred_element_type=jnp.float32)
        dk_piece = jnp.einsum("htn,thd->nd", ds_b, queries, preferred_element_type=jnp.float32)
        dv_piece = jnp.einsum("htn,thd->nd", p_b, grads3, preferred_element_type=jnp.float32)
        own = (
            dk_piece.reshape(per_block, tokens, head_dim),
            dv_piece.reshape(per_block, tokens, head_dim),
        )
        previous = own
        acc[b] = own if acc[b] is None else tuple(x + y for x, y in zip(own, acc[b]))
        for s_step in reversed(range(steps)):
            lo_block = 2 ** s_step // per_block
            if lo_block == 0:
                break
            if lo_block <= b < 2 * lo_block:
                recv = lax.ppermute(
                    tuple(x.astype(jnp.bfloat16) for x in acc[b]), "ctx", step_pairs(n, orders, s_step)
                )
                recv = tuple(r.astype(jnp.float32) for r in recv)
                dst = b - lo_block
                acc[dst] = recv if acc[dst] is None else tuple(
                    x + y for x, y in zip(acc[dst], recv)
                )
                acc[b] = None
                break
    last = acc[0]
    for s_step in reversed(range(steps)):
        half = 2 ** s_step
        if half >= per_block:
            continue
        recv = lax.ppermute(
            tuple(x[half : 2 * half].astype(jnp.bfloat16) for x in last),
            "ctx",
            step_pairs(n, orders, s_step),
        )
        last = tuple(x[:half] + r.astype(jnp.float32) for x, r in zip(last, recv))
    dk_mine, dv_mine = (x[0] for x in last)

    dq_b = dq.astype(jnp.bfloat16).reshape(tokens, heads * head_dim)
    query_part = lax.psum_scatter(
        contract_rows(dq_b, w_query).astype(jnp.bfloat16), "tp", scatter_dimension=1, tiled=True
    )
    kv_grad = jnp.concatenate([dk_mine, dv_mine], axis=1).astype(jnp.bfloat16)
    total = query_part.astype(jnp.float32) + contract_rows(kv_grad, my_kv_rows)
    for k in range(1, m):
        shift = [(j, (j + k) % m) for j in range(m)]
        total = total + contract_rows(lax.ppermute(kv_grad, "tp", shift), kv_rows_from[k])
    return total.astype(jnp.bfloat16)


def solution(mesh):
    placed = (
        P("ctx", None),
        P(None, "tp"),
        P(None, "tp"),
        P(None, "tp"),
        P("ctx", "tp"),
        P("ctx", "tp"),
        P(),
    )
    return jax.shard_map(
        on_device, mesh=mesh, in_specs=placed, out_specs=P("ctx", "tp"), check_vma=False
    )
```

```python
import math

import numpy as np

import jax
import jax.numpy as jnp
from jax import lax
from jax.sharding import PartitionSpec as P

big_negative = -1e30


def exchange_orders(n):
    if n == 64:
        return ([5, 3, 2, 4, 1, 0], [3, 2, 5, 1, 4, 0])
    bits = list(range(int(math.log2(n))))[::-1]
    return (bits, bits)


def step_pairs(n, orders, s):
    return [(i, i ^ (1 << orders[i & 1][s])) for i in range(n)]


def owner_table(n, orders):
    owners = [[i] for i in range(n)]
    for s in range(len(orders[0])):
        owners = [owners[i] + owners[j] for i, j in step_pairs(n, orders, s)]
    return np.asarray(owners, np.int32)


def gather_parts(pieces, n, orders):
    parts = [tuple(p[None] for p in pieces)]
    buf = parts[0]
    for s in range(len(orders[0])):
        other = lax.ppermute(buf, "ctx", step_pairs(n, orders, s))
        parts.append(other)
        if s + 1 < len(orders[0]):
            buf = tuple(jnp.concatenate([b, o], axis=0) for b, o in zip(buf, other))
    return parts


def slot_range(parts, lo, hi):
    picked = []
    for s, part in enumerate(parts):
        first = 0 if s == 0 else 2 ** (s - 1)
        size = part[0].shape[0]
        a, b = max(lo, first), min(hi, first + size)
        if a < b:
            picked.append(tuple(x[a - first : b - first] for x in part))
    if len(picked) == 1:
        return picked[0]
    return tuple(jnp.concatenate(xs, axis=0) for xs in zip(*picked))


def row_positions(order, start, count, span):
    rows = start + lax.iota(jnp.int32, count)
    slot = rows // span
    table = jnp.sum(
        jnp.where(slot[:, None] == lax.iota(jnp.int32, order.shape[0])[None, :], order[None, :], 0),
        axis=1,
    )
    return table * span + rows % span


def contract_rows(left, weight):
    return lax.dot_general(
        left, weight, (((1,), (1,)), ((), ())), preferred_element_type=jnp.float32
    )


def on_device(inputs, w_query, w_key, w_value, attn_out, d_out, block_order):
    tokens = inputs.shape[0]
    span = tokens // 2
    head_dim = w_key.shape[1]
    heads = w_query.shape[1] // head_dim
    scale = head_dim ** (-0.5)
    n = lax.axis_size("ctx")
    orders = exchange_orders(n)
    steps = len(orders[0])
    me = lax.axis_index("ctx")
    keys = jnp.dot(inputs, w_key, preferred_element_type=jnp.float32).astype(jnp.bfloat16)
    values = jnp.dot(inputs, w_value, preferred_element_type=jnp.float32).astype(jnp.bfloat16)
    seq = tokens * n
    my_pos = row_positions(block_order, me * tokens, tokens, span)
    queries = (
        jnp.dot(inputs, w_query, preferred_element_type=jnp.float32)
        .astype(jnp.bfloat16)
        .reshape(tokens, heads, head_dim)
    )
    grads3 = d_out.reshape(tokens, heads, head_dim)
    delta = jnp.sum(
        grads3.astype(jnp.float32) * attn_out.reshape(tokens, heads, head_dim).astype(jnp.float32),
        axis=-1,
    ).T

    owners = lax.dynamic_index_in_dim(jnp.asarray(owner_table(n, orders)), me, 0, keepdims=False)
    per_owner = tokens // span
    owner_blocks = (owners[:, None] * per_owner + lax.iota(jnp.int32, per_owner)[None, :]).reshape(-1)
    block_ids = jnp.sum(
        jnp.where(
            owner_blocks[:, None] == lax.iota(jnp.int32, block_order.shape[0])[None, :],
            block_order[None, :],
            0,
        ),
        axis=1,
    )
    all_pos = (block_ids[:, None] * span + lax.iota(jnp.int32, span)[None, :]).reshape(seq)

    m = lax.axis_size("tp")
    t = lax.axis_index("tp")
    cols = w_query.shape[0] // m
    kv_weights = jnp.concatenate([w_key, w_value], axis=1)
    my_kv_rows = lax.dynamic_slice_in_dim(kv_weights, t * cols, cols, 0)
    kv_rows_from = [None]
    for k in range(1, m):
        shift = [(j, (j + k) % m) for j in range(m)]
        sent = lax.dynamic_slice_in_dim(kv_weights, ((t + k) % m) * cols, cols, 0)
        kv_rows_from.append(lax.ppermute(sent, "tp", shift))
    swapped, queries = lax.optimization_barrier((tuple(kv_rows_from[1:]), queries))
    kv_rows_from = [None] + list(swapped)

    parts = gather_parts((keys, values), n, orders)
    block = math.gcd(seq, 1024)
    count = seq // block
    per_block = block // tokens

    def block_kv(b):
        k, v = slot_range(parts, b * per_block, (b + 1) * per_block)
        return k.reshape(block, head_dim), v.reshape(block, head_dim)

    def block_mask(b):
        key_pos = lax.slice_in_dim(all_pos, b * block, (b + 1) * block)
        return (key_pos[None, :] <= my_pos[:, None])[None]

    top = jnp.full((heads, tokens), big_negative, jnp.float32)
    total = jnp.zeros((heads, tokens), jnp.float32)
    stats_block = 2 * block if seq % (2 * block) == 0 else block
    per_stats = stats_block // tokens
    for b in range(seq // stats_block):
        (piece_k, _) = slot_range(parts, b * per_stats, (b + 1) * per_stats)
        piece_k = piece_k.reshape(stats_block, head_dim)
        key_pos = lax.slice_in_dim(all_pos, b * stats_block, (b + 1) * stats_block)
        mask = (key_pos[None, :] <= my_pos[:, None])[None]
        s = jnp.einsum("thd,nd->htn", queries, piece_k, preferred_element_type=jnp.float32) * scale
        s = jnp.where(mask, s, big_negative)
        top_new = jnp.maximum(top, jnp.max(s, axis=-1))
        terms = jnp.where(mask, jnp.exp(s - top_new[..., None]), 0.0)
        total = total * jnp.exp(top - top_new) + jnp.sum(terms, axis=-1)
        top = top_new
    lse = top + jnp.log(total)

    dq = jnp.zeros((tokens, heads, head_dim), jnp.float32)
    acc = [None] * count
    previous = None
    for b in reversed(range(count)):
        piece_k, piece_v = block_kv(b)
        if previous is not None:
            (piece_k, piece_v), _ = lax.optimization_barrier(((piece_k, piece_v), previous))
        mask = block_mask(b)
        s = jnp.einsum("thd,nd->htn", queries, piece_k, preferred_element_type=jnp.float32) * scale
        p = jnp.where(mask, jnp.exp(s - lse[..., None]), 0.0)
        dp = jnp.einsum("thd,nd->htn", grads3, piece_v, preferred_element_type=jnp.float32)
        ds_b = (p * (dp - delta[..., None]) * scale).astype(jnp.bfloat16)
        p_b = p.astype(jnp.bfloat16)
        dq = dq + jnp.einsum("htn,nd->thd", ds_b, piece_k, preferred_element_type=jnp.float32)
        dk_piece = jnp.einsum("htn,thd->nd", ds_b, queries, preferred_element_type=jnp.float32)
        dv_piece = jnp.einsum("htn,thd->nd", p_b, grads3, preferred_element_type=jnp.float32)
        own = (
            dk_piece.reshape(per_block, tokens, head_dim),
            dv_piece.reshape(per_block, tokens, head_dim),
        )
        previous = own
        acc[b] = own if acc[b] is None else tuple(x + y for x, y in zip(own, acc[b]))
        for s_step in reversed(range(steps)):
            lo_block = 2 ** s_step // per_block
            if lo_block == 0:
                break
            if lo_block <= b < 2 * lo_block:
                recv = lax.ppermute(
                    tuple(x.astype(jnp.bfloat16) for x in acc[b]), "ctx", step_pairs(n, orders, s_step)
                )
                recv = tuple(r.astype(jnp.float32) for r in recv)
                dst = b - lo_block
                acc[dst] = recv if acc[dst] is None else tuple(
                    x + y for x, y in zip(acc[dst], recv)
                )
                acc[b] = None
                break
    last = acc[0]
    for s_step in reversed(range(steps)):
        half = 2 ** s_step
        if half >= per_block:
            continue
        recv = lax.ppermute(
            tuple(x[half : 2 * half].astype(jnp.bfloat16) for x in last),
            "ctx",
            step_pairs(n, orders, s_step),
        )
        last = tuple(x[:half] + r.astype(jnp.float32) for x, r in zip(last, recv))
    dk_mine, dv_mine = (x[0] for x in last)

    dq_b = dq.astype(jnp.bfloat16).reshape(tokens, heads * head_dim)
    query_part = lax.psum_scatter(
        contract_rows(dq_b, w_query).astype(jnp.bfloat16), "tp", scatter_dimension=1, tiled=True
    )
    kv_grad = jnp.concatenate([dk_mine, dv_mine], axis=1).astype(jnp.bfloat16)
    total = query_part.astype(jnp.float32) + contract_rows(kv_grad, my_kv_rows)
    for k in range(1, m):
        shift = [(j, (j + k) % m) for j in range(m)]
        total = total + contract_rows(lax.ppermute(kv_grad, "tp", shift), kv_rows_from[k])
    return total.astype(jnp.bfloat16)


def solution(mesh):
    placed = (
        P("ctx", None),
        P(None, "tp"),
        P(None, "tp"),
        P(None, "tp"),
        P("ctx", "tp"),
        P("ctx", "tp"),
        P(),
    )
    return jax.shard_map(
        on_device, mesh=mesh, in_specs=placed, out_specs=P("ctx", "tp"), check_vma=False
    )
```
